512 devices in a mesh: expert: 64 (over x_hi, z, core), dp: 8 (over x_lo, y).
Axes of the slice: x: 4 (x_hi: 2, x_lo: 2; x = x_hi * 2 + x_lo), y: 4, z: 16, core: 2. Of those that a mesh axis runs over, the one named last changes fastest.
Arguments:
- skip_stream: bfloat16 [4096, 4096], P(('expert', 'dp')), may hold values from -6 to 6
- attention_probes: bfloat16 [4096, 4096], P(('expert', 'dp')), may hold values from -5 to 5
- stored_attention_lookups: bfloat16 [4096, 16, 512], P(('expert', 'dp')), may hold values from -5 to 5
- stored_attention_contents: bfloat16 [4096, 16, 512], P(('expert', 'dp')), may hold values from -6 to 6
- incoming_lookup_entries: bfloat16 [4096, 512], P(('expert', 'dp')), may hold values from -6 to 6
- incoming_content_entries: bfloat16 [4096, 512], P(('expert', 'dp')), may hold values from -6 to 6
- filled_slot_spans: int32 [4096], P(('expert', 'dp')), may hold values from 2 to 16, as said below
- layernorm_gain: float32 [4096], replicated, may hold values from 0.1 to 1.9
- routed_specialist_indices: int32 [4096, 8], P(('expert', 'dp')), may hold values from 0 to 63, all different within a row; in each aligned block of 8 rows (0 to 7, 8 to 15, ...) at most 2 rows name the same one
- routing_probabilities: float32 [4096, 8], P(('expert', 'dp')), may hold values from 0.05 to 1
- admission_limits: int32 [64], replicated, may hold values from 256 to 1024
- swap_indicator: int32 [64], replicated, may hold values from 0 to 1, as said below
- gating_projection_matrix: bfloat16 [64, 768, 4096], P('expert', 'dp'), may hold values from -0.09375 to 0.09375
- widening_projection_matrix: bfloat16 [64, 768, 4096], P('expert', 'dp'), may hold values from -0.09375 to 0.09375
- output_projection_matrix: bfloat16 [64, 768, 4096], P('expert', None, 'dp'), may hold values from -0.21875 to 0.21875
Outputs:
- layer_out: bfloat16 [4096, 4096], P(('expert', 'dp'))
- device_share: float32 [64], P('expert')
- held_gate: bfloat16 [64, 768, 4096], P('expert', 'dp')
- held_up: bfloat16 [64, 768, 4096], P('expert', 'dp')
- held_down: bfloat16 [64, 768, 4096], P('expert', None, 'dp')
The draws below stay inside these ranges and needn't reach their ends.
Inputs may be any that keep to these rules, and one draw needn't show every extreme that they name: `filled_slot_spans`: each sequence has 2 or more valid slots and some sequence has all 16. `routed_specialist_indices`: in each aligned block of 8 rows (the rows of one device) no expert is named by more than 2 rows; the entries of a row differ. swap_indicator[i] equals swap_indicator[i + 32].
All inputs are finite; a program needn't handle non-finite values.
Results may differ from the reference program's by a relative error of at most 0.017.
Values may be sent and summed in bfloat16 or wider, within the bound.
No kernel may reach another device: no remote copies, remote signals or barrier semaphores. Data moves between devices by JAX's collectives and lax.ppermute only.
A program may use at most 64 MiB of HBM per device.

```python
import math
import jax
import jax.numpy as jnp
import numpy as np
from jax import lax

D = 4096
QH = 32
KVH = 4
HEAD = 128
EXPERT_FF = 768
ROUTED_PER_TOKEN = 8
LEN = 16
LOCAL_STREAMS = 8
SPECIALIST_NUM = 64
CAP = 2
GLOBAL_STREAMS = 4096
DEVICES = 512


def drawn_fields(key):
    query_key = jax.random.fold_in(key, 11)
    cache_key = jax.random.fold_in(key, 12)
    query_part = jnp.clip(jax.random.normal(query_key, (GLOBAL_STREAMS, QH * HEAD), jnp.float32), -5.0, 5.0)
    cache_part = jnp.clip(jax.random.normal(cache_key, (GLOBAL_STREAMS, LEN, KVH * HEAD), jnp.float32), -5.0, 5.0)
    return (query_part, cache_part)


def draw_attention_probes(key, part):
    return drawn_fields(key)[0].astype(jnp.bfloat16)


def draw_stored_attention_lookups(key, part):
    return drawn_fields(key)[1].astype(jnp.bfloat16)


def draw_filled_slot_spans(key, part):
    values = jax.random.randint(jax.random.fold_in(key, 21), (GLOBAL_STREAMS,), 2, LEN + 1)
    return values.at[0].set(LEN).astype(jnp.int32)


def draw_swap_indicator(key, part):
    first_half = jax.random.randint(jax.random.fold_in(key, 31), (SPECIALIST_NUM // 2,), 0, 2)
    first_half = first_half.at[0].set(1).at[1].set(0)
    return jnp.concatenate([first_half, first_half]).astype(jnp.int32)


def touch_ends(result, key, low, high):
    spot = [jax.random.randint(jax.random.fold_in(key, axis), (), 0, length) for axis, length in enumerate(result.shape)]
    longest = result.shape.index(max(result.shape))
    next_to = spot[:longest] + [(spot[longest] + 1) % result.shape[longest]] + spot[longest + 1:]
    return result.at[tuple(spot)].set(low).at[tuple(next_to)].set(high)


def level_of(stream_key, shape, shards, smallest, top_value):
    level = 1.0
    for axis_at, blocks in shards:
        draws = jax.random.uniform(jax.random.fold_in(jax.random.fold_in(stream_key, 6), axis_at), (blocks,), jnp.float32, smallest / len(shards), top_value / len(shards))
        level = level * jnp.repeat(jnp.exp(draws), shape[axis_at] // blocks).reshape((-1,) + (1,) * (len(shape) - 1 - axis_at))
    return level


def shared_out(key, own, number, rows, count, top, bound, slope):
    sequence = jax.random.permutation(key, count)
    heavy_load, ordinary = load_shares(count, rows * top, bound, slope, True), load_shares(count, rows * top, bound, slope, False)
    places = jnp.arange(count)

    def named(lengths, turn):
        used = int((lengths > 0).sum())
        fixed = max(1, used // 4)
        moved = fixed + (places - fixed + turn * (used - fixed)) % max(1, count - fixed)
        return jnp.zeros((count,), jnp.int32).at[sequence[jnp.where(places < fixed, places, moved)]].set(jnp.asarray(lengths, jnp.int32))

    lengths = jnp.where(number % 4 == 0, named(heavy_load, number // 4), named(ordinary, number - number // 4 - 1))
    mixed = jax.random.permutation(jax.random.fold_in(own, 3), count)
    source_of, sink = mixed[0:count // 2 * 2:2], mixed[1:count // 2 * 2:2]
    room = jnp.minimum(lengths[source_of] - 1, bound - lengths[sink]) // 2
    room = jnp.where((source_of == sequence[0]) | (sink == sequence[0]) | (lengths[sink] == 0), 0, jnp.maximum(room, 0))
    moved = jax.random.randint(jax.random.fold_in(own, 4), (count // 2,), 0, 1 << 20) % (room + 1)
    lengths = lengths.at[source_of].add(-moved).at[sink].add(moved)
    labels = jnp.searchsorted(jnp.cumsum(lengths), jnp.arange(rows * top), side="right").astype(jnp.int32)
    table = labels.reshape(top, rows).T
    table = table[jax.random.permutation(jax.random.fold_in(own, 1), rows)]
    turn = jax.random.randint(jax.random.fold_in(own, 2), (rows, 1), 0, top)
    return jnp.take_along_axis(table, (jnp.arange(top)[None, :] + turn) % top, axis=1)


def load_shares(count, total, limit, lean, full):
    portions = [(1 << 20) // math.isqrt(grade ** lean) + 1 for grade in range(1, count + 1)]
    largest = limit if full else min(limit, max(-(-total // count), total * portions[0] // sum(portions)))
    least = 1 if total - largest >= count - 1 else 0
    holding, surplus = [largest] + [least] * (count - 1), total - largest - least * (count - 1)
    while surplus > 0:
        free = [i for i in range(1, count) if holding[i] < largest] or [i for i in range(1, count) if holding[i] < limit]
        pool, remaining = sum([portions[i] for i in free]), surplus
        for i in free:
            addition = min(limit - holding[i], max(1, remaining * portions[i] // pool), surplus)
            holding[i] = holding[i] + addition
            surplus = surplus - addition
    return np.array(holding)


def noise(own_key, extent, deviation, limit, pieces=(), held_as=jnp.bfloat16):
    result = jax.random.normal(own_key, extent, jnp.float32) * deviation
    if len(pieces) > 0:
        result = level_of(own_key, extent, pieces, -0.22, 0.18) * result
    return jnp.clip(result, min=-limit, max=limit).astype(held_as)


def setup_inputs(seed: int = 0) -> dict:
    key_of = jax.random.split(jax.random.key(seed), 16)
    skip_stream = noise(key_of[0], (GLOBAL_STREAMS, D), 1.0, 6.0, ((0, 512),))
    attention_probes = draw_attention_probes(jax.random.fold_in(key_of[15], 71), 0)
    stored_attention_lookups = draw_stored_attention_lookups(jax.random.fold_in(key_of[15], 71), 0)
    stored_attention_contents = noise(key_of[3], (GLOBAL_STREAMS, LEN, KVH * HEAD), 1.0, 6.0, ((0, 512),))
    incoming_lookup_entries = noise(key_of[4], (GLOBAL_STREAMS, KVH * HEAD), 1.0, 6.0, ((0, 512),))
    incoming_content_entries = noise(key_of[5], (GLOBAL_STREAMS, KVH * HEAD), 1.0, 6.0, ((0, 512),))
    filled_slot_spans = draw_filled_slot_spans(jax.random.fold_in(key_of[15], 71), 0)
    layernorm_gain = jnp.clip(1.0 + 0.18 * jax.random.normal(key_of[7], (D,), jnp.float32), 0.1, 1.9)
    routed_specialist_indices_keys = jax.random.split(jax.random.fold_in(key_of[8], 1), GLOBAL_STREAMS // LOCAL_STREAMS)
    routed_specialist_indices_turns = jax.random.permutation(jax.random.fold_in(key_of[8], 3), GLOBAL_STREAMS // LOCAL_STREAMS)
    routed_specialist_indices = jax.vmap(lambda own, number: shared_out(jax.random.fold_in(key_of[8], 2), own, number, LOCAL_STREAMS, SPECIALIST_NUM, ROUTED_PER_TOKEN, CAP, 2))(routed_specialist_indices_keys, routed_specialist_indices_turns).reshape((GLOBAL_STREAMS, ROUTED_PER_TOKEN))
    routing_probabilities = jnp.clip(0.05 + 0.95 * jax.random.uniform(key_of[9], (GLOBAL_STREAMS, ROUTED_PER_TOKEN), jnp.float32) ** level_of(key_of[9], (GLOBAL_STREAMS, ROUTED_PER_TOKEN), ((0, 512),), -0.2, 0.2), 0.05, 1.0)
    admission_limits = touch_ends(jax.random.randint(key_of[10], (SPECIALIST_NUM,), LOCAL_STREAMS * DEVICES * ROUTED_PER_TOKEN // (2 * SPECIALIST_NUM), 2 * LOCAL_STREAMS * DEVICES * ROUTED_PER_TOKEN // SPECIALIST_NUM + 1), jax.random.fold_in(key_of[10], 1), LOCAL_STREAMS * DEVICES * ROUTED_PER_TOKEN // (2 * SPECIALIST_NUM), (2 * LOCAL_STREAMS * DEVICES * ROUTED_PER_TOKEN // SPECIALIST_NUM + 1) - 1).astype(jnp.int32)
    swap_indicator = draw_swap_indicator(jax.random.fold_in(key_of[15], 71), 0)
    gating_projection_matrix = noise(key_of[12], (SPECIALIST_NUM, EXPERT_FF, D), D ** -0.5, 0.09375, ((0, 64), (1, 8)))
    widening_projection_matrix = noise(key_of[13], (SPECIALIST_NUM, EXPERT_FF, D), D ** -0.5, 0.09375, ((0, 64), (1, 8)))
    output_projection_matrix = noise(key_of[14], (SPECIALIST_NUM, EXPERT_FF, D), EXPERT_FF ** -0.5, 0.21875, ((0, 64), (2, 8)))
    return {"skip_stream": skip_stream, "attention_probes": attention_probes, "stored_attention_lookups": stored_attention_lookups, "stored_attention_contents": stored_attention_contents, "incoming_lookup_entries": incoming_lookup_entries, "incoming_content_entries": incoming_content_entries, "filled_slot_spans": filled_slot_spans, "layernorm_gain": layernorm_gain, "routed_specialist_indices": routed_specialist_indices, "routing_probabilities": routing_probabilities, "admission_limits": admission_limits, "swap_indicator": swap_indicator, "gating_projection_matrix": gating_projection_matrix, "widening_projection_matrix": widening_projection_matrix, "output_projection_matrix": output_projection_matrix}


def attention(parts):
    query_rows, key_rows, value_rows, new_key, new_value, valid_len = parts
    seq_count = query_rows.shape[0]
    cache_len = key_rows.shape[1]
    group = QH // KVH
    scale = HEAD ** (-0.5)
    query_view = query_rows.astype(jnp.float32).reshape(seq_count, KVH, group, HEAD)
    key_view = key_rows.astype(jnp.float32).reshape(seq_count, cache_len, KVH, HEAD)
    value_view = value_rows.astype(jnp.float32).reshape(seq_count, cache_len, KVH, HEAD)
    scores = jnp.einsum('skgd,slkd->skgl', query_view, key_view) * scale
    valid = jnp.arange(cache_len, dtype=jnp.int32)[None, :] < valid_len[:, None]
    scores = jnp.where(valid[:, None, None, :], scores, -1e+30)
    own_score = jnp.einsum('skgd,skd->skg', query_view, new_key.astype(jnp.float32).reshape(seq_count, KVH, HEAD)) * scale
    highest = jnp.maximum(lax.optimization_barrier(jnp.max(scores, axis=-1)), own_score)
    weights = jnp.exp(scores - highest[..., None])
    own_weight = jnp.exp(own_score - highest)
    denom = lax.optimization_barrier(jnp.sum(weights, axis=-1)) + own_weight
    probs = (weights / denom[..., None]).astype(jnp.bfloat16)
    own_prob = (own_weight / denom).astype(jnp.bfloat16)
    mixed = jnp.einsum('skgl,slkd->skgd', probs.astype(jnp.float32), value_view)
    mixed = mixed + own_prob.astype(jnp.float32)[..., None] * new_value.astype(jnp.float32).reshape(seq_count, KVH, 1, HEAD)
    return mixed.reshape(seq_count, QH * HEAD).astype(jnp.bfloat16)

def reference(skip_stream, attention_probes, stored_attention_lookups, stored_attention_contents, incoming_lookup_entries, incoming_content_entries, filled_slot_spans, layernorm_gain, routed_specialist_indices, routing_probabilities, admission_limits, swap_indicator, gating_projection_matrix, widening_projection_matrix, output_projection_matrix):
    blocks = GLOBAL_STREAMS // LOCAL_STREAMS
    attn = lax.map(attention, (attention_probes.reshape(blocks, LOCAL_STREAMS, D), stored_attention_lookups.reshape(blocks, LOCAL_STREAMS, LEN, KVH * HEAD), stored_attention_contents.reshape(blocks, LOCAL_STREAMS, LEN, KVH * HEAD), incoming_lookup_entries.reshape(blocks, LOCAL_STREAMS, KVH * HEAD), incoming_content_entries.reshape(blocks, LOCAL_STREAMS, KVH * HEAD), filled_slot_spans.reshape(blocks, LOCAL_STREAMS)))
    attn = attn.reshape(GLOBAL_STREAMS, D)
    stream = skip_stream.astype(jnp.float32) + attn.astype(jnp.float32)
    normed = (stream * lax.rsqrt(lax.optimization_barrier(jnp.mean(stream * stream, axis=-1, keepdims=True)) + 1e-06) * layernorm_gain).astype(jnp.bfloat16)
    expert_range = jnp.arange(SPECIALIST_NUM, dtype=jnp.int32)
    route_hot = (routed_specialist_indices[:, :, None] == expert_range[None, None, :]).astype(jnp.int32)
    row_hot = lax.optimization_barrier(jnp.sum(route_hot, axis=1))
    earlier = jnp.cumsum(row_hot, axis=0) - row_hot
    pair_rank = lax.optimization_barrier(jnp.sum(route_hot * earlier[:, None, :], axis=-1)).astype(jnp.int32)
    specialist_tallies = lax.optimization_barrier(jnp.sum(row_hot, axis=0))
    paired_limit = jnp.take(admission_limits, routed_specialist_indices)
    kept = pair_rank < paired_limit
    slot_bound = 2 * GLOBAL_STREAMS * ROUTED_PER_TOKEN // SPECIALIST_NUM
    row_index = jnp.repeat(jnp.arange(GLOBAL_STREAMS, dtype=jnp.int32), ROUTED_PER_TOKEN)
    source_rows = jnp.full((SPECIALIST_NUM, slot_bound), GLOBAL_STREAMS, jnp.int32).at[routed_specialist_indices.reshape(-1), pair_rank.reshape(-1)].set(row_index, mode='drop')
    normed_pad = jnp.concatenate([normed, jnp.zeros((1, D), jnp.bfloat16)], axis=0)

    def expert_rows(parts):
        picks, gate_mat, up_mat, down_mat = parts
        rows_in = normed_pad[picks]
        gate_val = jnp.dot(rows_in, gate_mat.T, preferred_element_type=jnp.float32)
        up_val = jnp.dot(rows_in, up_mat.T, preferred_element_type=jnp.float32)
        hidden_val = (jax.nn.silu(gate_val) * up_val).astype(jnp.bfloat16)
        return jnp.dot(hidden_val, down_mat, preferred_element_type=jnp.float32).astype(jnp.bfloat16)
    outputs = lax.map(expert_rows, (source_rows, gating_projection_matrix, widening_projection_matrix, output_projection_matrix))
    expert_mix = jnp.zeros((GLOBAL_STREAMS, D), jnp.float32)
    for choice_k in range(ROUTED_PER_TOKEN):
        picked = outputs[routed_specialist_indices[:, choice_k], jnp.minimum(pair_rank[:, choice_k], slot_bound - 1)]
        factor = jnp.where(kept[:, choice_k], routing_probabilities[:, choice_k], 0.0)
        expert_mix = expert_mix + factor[:, None] * picked.astype(jnp.float32)
    layer_out = (stream + expert_mix).astype(jnp.bfloat16)
    retained_specialist = jnp.where(swap_indicator == 1, (expert_range + SPECIALIST_NUM // 2) % SPECIALIST_NUM, expert_range).astype(jnp.int32)
    held_gate = jnp.take(gating_projection_matrix, retained_specialist, axis=0)
    held_up = jnp.take(widening_projection_matrix, retained_specialist, axis=0)
    held_down = jnp.take(output_projection_matrix, retained_specialist, axis=0)
    handled_specialist = jnp.minimum(specialist_tallies, admission_limits).astype(jnp.float32) / (GLOBAL_STREAMS * ROUTED_PER_TOKEN / SPECIALIST_NUM)
    device_share = jnp.take(handled_specialist, retained_specialist)
    return (layer_out, device_share, held_gate, held_up, held_down)
```

```python
import jax
import jax.numpy as jnp
from jax import lax
from jax.sharding import PartitionSpec as P

QH = 32
KVH = 4
HEAD = 128


def swapped(value, axis, stride):
    mask = 2**stride
    pairs = [(source, source ^ mask) for source in range(lax.axis_size(axis))]
    return lax.ppermute(value, axis, pairs)


def attention(query_rows, key_rows, value_rows, new_key, new_value, valid_len):
    seq_count = query_rows.shape[0]
    cache_len = key_rows.shape[1]
    group = QH // KVH
    scale = HEAD ** (-0.5)
    query_view = query_rows.reshape(seq_count, KVH, group, HEAD)
    key_view = key_rows.reshape(seq_count, cache_len, KVH, HEAD)
    value_view = value_rows.reshape(seq_count, cache_len, KVH, HEAD)
    scores = (
        jnp.einsum("skgd,slkd->skgl", query_view, key_view, preferred_element_type=jnp.float32)
        * scale
    )
    valid = lax.broadcasted_iota(jnp.int32, (seq_count, cache_len), 1) < valid_len[:, None]
    scores = jnp.where(valid[:, None, None, :], scores, -1e30)
    own_score = (
        jnp.einsum(
            "skgd,skd->skg",
            query_view,
            new_key.reshape(seq_count, KVH, HEAD),
            preferred_element_type=jnp.float32,
        )
        * scale
    )
    highest = jnp.maximum(jnp.max(scores, axis=-1), own_score)
    weights = jnp.exp(scores - highest[..., None])
    own_weight = jnp.exp(own_score - highest)
    denom = jnp.sum(weights, axis=-1) + own_weight
    probs = (weights / denom[..., None]).astype(jnp.bfloat16)
    own_prob = (own_weight / denom).astype(jnp.bfloat16)
    mixed = jnp.einsum("skgl,slkd->skgd", probs, value_view, preferred_element_type=jnp.float32)
    mixed = mixed + own_prob.astype(jnp.float32)[..., None] * new_value.reshape(
        seq_count, KVH, 1, HEAD
    ).astype(jnp.float32)
    return mixed.reshape(seq_count, QH * HEAD).astype(jnp.bfloat16)


def per_device(
    skip_stream,
    attention_probes,
    stored_attention_lookups,
    stored_attention_contents,
    incoming_lookup_entries,
    incoming_content_entries,
    filled_slot_spans,
    layernorm_gain,
    routed_specialist_indices,
    routing_probabilities,
    admission_limits,
    swap_indicator,
    gating_projection_matrix,
    widening_projection_matrix,
    output_projection_matrix,
):
    experts = lax.axis_size("expert")
    groups = lax.axis_size("dp")
    half_axis = experts // 2
    far_bit = experts.bit_length() - 2
    my_index = lax.axis_index("expert")
    my_device = my_index * groups + lax.axis_index("dp")
    own_weights = (
        gating_projection_matrix[0],
        widening_projection_matrix[0],
        output_projection_matrix[0],
    )
    partner = swapped(own_weights, "expert", far_bit)
    take_other = swap_indicator[my_index] == 1
    gate_held = jnp.where(take_other, partner[0], own_weights[0])
    up_held = jnp.where(take_other, partner[1], own_weights[1])
    down_held = jnp.where(take_other, partner[2], own_weights[2])
    retained_specialist = jnp.where(take_other, (my_index + half_axis) % experts, my_index)

    seq_rows = skip_stream.shape[0]
    top_count = routed_specialist_indices.shape[1]
    width = skip_stream.shape[1]
    slot_cap = 2
    expert_range = lax.broadcasted_iota(jnp.int32, (experts,), 0)

    all_routes = lax.all_gather(routed_specialist_indices, ("expert", "dp"), axis=0, tiled=True)
    all_hot = jnp.sum(
        (all_routes[:, :, None] == expert_range[None, None, :]).astype(jnp.int32), axis=1
    )
    all_rows = lax.broadcasted_iota(jnp.int32, (all_routes.shape[0], 1), 0)
    before_mine = jnp.sum(jnp.where(all_rows < my_device * seq_rows, all_hot, 0), axis=0)
    tallies = jnp.sum(all_hot, axis=0)

    route_hot = (routed_specialist_indices[:, :, None] == expert_range[None, None, :]).astype(
        jnp.int32
    )
    row_hot = jnp.sum(route_hot, axis=1)
    earlier = jnp.cumsum(row_hot, axis=0) - row_hot
    local_rank = jnp.sum(route_hot * earlier[:, None, :], axis=-1)
    global_rank = local_rank + jnp.sum(route_hot * before_mine[None, None, :], axis=-1)
    pair_limit = jnp.sum(route_hot * admission_limits[None, None, :], axis=-1)
    kept = global_rank < pair_limit
    held_tally = jnp.sum(jnp.where(expert_range == retained_specialist, tallies, 0))
    device_share = jnp.minimum(held_tally, admission_limits[retained_specialist]).astype(
        jnp.float32
    ) / (seq_rows * top_count * groups)

    attn = attention(
        attention_probes,
        stored_attention_lookups,
        stored_attention_contents,
        incoming_lookup_entries,
        incoming_content_entries,
        filled_slot_spans,
    )
    stream = skip_stream.astype(jnp.float32) + attn.astype(jnp.float32)
    normed = (
        stream
        * lax.rsqrt(jnp.mean(stream * stream, axis=-1, keepdims=True) + 1e-06)
        * layernorm_gain
    ).astype(jnp.bfloat16)

    slot_code = routed_specialist_indices * slot_cap + local_rank
    targets = lax.broadcasted_iota(jnp.int32, (experts * slot_cap,), 0)
    slot_hits = jnp.any(slot_code[:, :, None] == targets[None, None, :], axis=1)
    occupied = jnp.any(slot_hits, axis=0)
    row_range = lax.broadcasted_iota(jnp.int32, (seq_rows, 1), 0)
    source_row = jnp.sum(jnp.where(slot_hits, row_range, 0), axis=0) + jnp.where(
        occupied, 0, seq_rows
    )
    padded_rows = jnp.concatenate([normed, jnp.zeros((1, width), jnp.bfloat16)], axis=0)
    outgoing = padded_rows[source_row].reshape(experts, slot_cap, width)
    arrived_rows = lax.all_to_all(outgoing, "expert", split_axis=0, concat_axis=0, tiled=True)
    column_rows = lax.all_gather(arrived_rows, "dp", axis=1, tiled=True)
    gate_val = jnp.einsum(
        "esf,hf->esh", column_rows, own_weights[0], preferred_element_type=jnp.float32
    )
    up_val = jnp.einsum(
        "esf,hf->esh", column_rows, own_weights[1], preferred_element_type=jnp.float32
    )
    hidden = (jax.nn.silu(gate_val) * up_val).astype(jnp.bfloat16)
    feature_cols = own_weights[2].shape[1]
    summed = jnp.einsum(
        "esn,nf->esf",
        lax.all_gather(hidden, "dp", axis=2, tiled=True),
        own_weights[2],
        preferred_element_type=jnp.float32,
    )
    results = summed.astype(jnp.bfloat16).reshape(experts, groups, slot_cap, feature_cols)
    returned = lax.all_to_all(
        lax.all_to_all(results, "expert", split_axis=0, concat_axis=0, tiled=True),
        "dp",
        split_axis=1,
        concat_axis=3,
        tiled=True,
    )
    returned_flat = returned.reshape(experts * slot_cap, width)
    picked = returned_flat[slot_code]
    factor = jnp.where(kept, routing_probabilities, 0.0)
    expert_mix = jnp.sum(factor[:, :, None] * picked.astype(jnp.float32), axis=1)
    layer_out = (stream + expert_mix).astype(jnp.bfloat16)
    return (layer_out, device_share.reshape(1), gate_held[None], up_held[None], down_held[None])


def solution(mesh):
    in_specs = (
        P(("expert", "dp"), None),
        P(("expert", "dp"), None),
        P(("expert", "dp"), None, None),
        P(("expert", "dp"), None, None),
        P(("expert", "dp"), None),
        P(("expert", "dp"), None),
        P(("expert", "dp")),
        P(),
        P(("expert", "dp"), None),
        P(("expert", "dp"), None),
        P(),
        P(),
        P("expert", "dp", None),
        P("expert", "dp", None),
        P("expert", None, "dp"),
    )
    out_specs = (
        P(("expert", "dp"), None),
        P("expert"),
        P("expert", "dp", None),
        P("expert", "dp", None),
        P("expert", None, "dp"),
    )
    return jax.shard_map(
        per_device, mesh=mesh, in_specs=in_specs, out_specs=out_specs, check_vma=False
    )
```

```python
import jax
import jax.numpy as jnp
from jax import lax
from jax.sharding import PartitionSpec as P

QH = 32
KVH = 4
HEAD = 128


def swapped(value, axis, stride):
    mask = 2**stride
    pairs = [(source, source ^ mask) for source in range(lax.axis_size(axis))]
    return lax.ppermute(value, axis, pairs)


def attention(query_rows, key_rows, value_rows, new_key, new_value, valid_len):
    seq_count = query_rows.shape[0]
    cache_len = key_rows.shape[1]
    group = QH // KVH
    scale = HEAD ** (-0.5)
    query_view = query_rows.reshape(seq_count, KVH, group, HEAD)
    key_view = key_rows.reshape(seq_count, cache_len, KVH, HEAD)
    value_view = value_rows.reshape(seq_count, cache_len, KVH, HEAD)
    scores = (
        jnp.einsum("skgd,slkd->skgl", query_view, key_view, preferred_element_type=jnp.float32)
        * scale
    )
    valid = lax.broadcasted_iota(jnp.int32, (seq_count, cache_len), 1) < valid_len[:, None]
    scores = jnp.where(valid[:, None, None, :], scores, -1e30)
    own_score = (
        jnp.einsum(
            "skgd,skd->skg",
            query_view,
            new_key.reshape(seq_count, KVH, HEAD),
            preferred_element_type=jnp.float32,
        )
        * scale
    )
    highest = jnp.maximum(jnp.max(scores, axis=-1), own_score)
    weights = jnp.exp(scores - highest[..., None])
    own_weight = jnp.exp(own_score - highest)
    denom = jnp.sum(weights, axis=-1) + own_weight
    probs = (weights / denom[..., None]).astype(jnp.bfloat16)
    own_prob = (own_weight / denom).astype(jnp.bfloat16)
    mixed = jnp.einsum("skgl,slkd->skgd", probs, value_view, preferred_element_type=jnp.float32)
    mixed = mixed + own_prob.astype(jnp.float32)[..., None] * new_value.reshape(
        seq_count, KVH, 1, HEAD
    ).astype(jnp.float32)
    return mixed.reshape(seq_count, QH * HEAD).astype(jnp.bfloat16)


def per_device(
    skip_stream,
    attention_probes,
    stored_attention_lookups,
    stored_attention_contents,
    incoming_lookup_entries,
    incoming_content_entries,
    filled_slot_spans,
    layernorm_gain,
    routed_specialist_indices,
    routing_probabilities,
    admission_limits,
    swap_indicator,
    gating_projection_matrix,
    widening_projection_matrix,
    output_projection_matrix,
):
    experts = lax.axis_size("expert")
    groups = lax.axis_size("dp")
    half_axis = experts // 2
    far_bit = experts.bit_length() - 2
    my_index = lax.axis_index("expert")
    my_device = my_index * groups + lax.axis_index("dp")
    own_weights = (
        gating_projection_matrix[0],
        widening_projection_matrix[0],
        output_projection_matrix[0],
    )
    partner = swapped(own_weights, "expert", far_bit)
    take_other = swap_indicator[my_index] == 1
    gate_held = jnp.where(take_other, partner[0], own_weights[0])
    up_held = jnp.where(take_other, partner[1], own_weights[1])
    down_held = jnp.where(take_other, partner[2], own_weights[2])
    retained_specialist = jnp.where(take_other, (my_index + half_axis) % experts, my_index)

    seq_rows = skip_stream.shape[0]
    top_count = routed_specialist_indices.shape[1]
    width = skip_stream.shape[1]
    slot_cap = 2
    expert_range = lax.broadcasted_iota(jnp.int32, (experts,), 0)

    route_hot = (routed_specialist_indices[:, :, None] == expert_range[None, None, :]).astype(
        jnp.int32
    )
    row_hot = jnp.sum(route_hot, axis=1)
    local_hist = jnp.sum(row_hot, axis=0).astype(jnp.bfloat16)
    all_hist = lax.all_gather(local_hist[None], ("expert", "dp"), axis=0, tiled=True)
    all_hist = all_hist.astype(jnp.int32)
    device_range = lax.broadcasted_iota(jnp.int32, (all_hist.shape[0], 1), 0)
    before_mine = jnp.sum(jnp.where(device_range < my_device, all_hist, 0), axis=0)
    tallies = jnp.sum(all_hist, axis=0)
    earlier = jnp.cumsum(row_hot, axis=0) - row_hot
    local_rank = jnp.sum(route_hot * earlier[:, None, :], axis=-1)
    global_rank = local_rank + jnp.sum(route_hot * before_mine[None, None, :], axis=-1)
    pair_limit = jnp.sum(route_hot * admission_limits[None, None, :], axis=-1)
    kept = global_rank < pair_limit
    held_tally = jnp.sum(jnp.where(expert_range == retained_specialist, tallies, 0))
    device_share = jnp.minimum(held_tally, admission_limits[retained_specialist]).astype(
        jnp.float32
    ) / (seq_rows * top_count * groups)

    attn = attention(
        attention_probes,
        stored_attention_lookups,
        stored_attention_contents,
        incoming_lookup_entries,
        incoming_content_entries,
        filled_slot_spans,
    )
    stream = skip_stream.astype(jnp.float32) + attn.astype(jnp.float32)
    normed = (
        stream
        * lax.rsqrt(jnp.mean(stream * stream, axis=-1, keepdims=True) + 1e-06)
        * layernorm_gain
    ).astype(jnp.bfloat16)

    slot_code = routed_specialist_indices * slot_cap + local_rank
    targets = lax.broadcasted_iota(jnp.int32, (experts * slot_cap,), 0)
    slot_hits = jnp.any(slot_code[:, :, None] == targets[None, None, :], axis=1)
    occupied = jnp.any(slot_hits, axis=0)
    row_range = lax.broadcasted_iota(jnp.int32, (seq_rows, 1), 0)
    source_row = jnp.sum(jnp.where(slot_hits, row_range, 0), axis=0) + jnp.where(
        occupied, 0, seq_rows
    )
    padded_rows = jnp.concatenate([normed, jnp.zeros((1, width), jnp.bfloat16)], axis=0)
    outgoing = padded_rows[source_row].reshape(experts, slot_cap, width)
    arrived_rows = lax.all_to_all(outgoing, "expert", split_axis=0, concat_axis=0, tiled=True)
    column_rows = lax.all_gather(arrived_rows, "dp", axis=1, tiled=True)
    gate_val = jnp.einsum(
        "esf,hf->esh", column_rows, own_weights[0], preferred_element_type=jnp.float32
    )
    up_val = jnp.einsum(
        "esf,hf->esh", column_rows, own_weights[1], preferred_element_type=jnp.float32
    )
    hidden = (jax.nn.silu(gate_val) * up_val).astype(jnp.bfloat16)
    feature_cols = own_weights[2].shape[1]
    summed = jnp.einsum(
        "esn,nf->esf",
        lax.all_gather(hidden, "dp", axis=2, tiled=True),
        own_weights[2],
        preferred_element_type=jnp.float32,
    )
    results = summed.astype(jnp.bfloat16).reshape(experts, groups, slot_cap, feature_cols)
    returned = lax.all_to_all(
        lax.all_to_all(results, "expert", split_axis=0, concat_axis=0, tiled=True),
        "dp",
        split_axis=1,
        concat_axis=3,
        tiled=True,
    )
    returned_flat = returned.reshape(experts * slot_cap, width)
    picked = returned_flat[slot_code]
    factor = jnp.where(kept, routing_probabilities, 0.0)
    expert_mix = jnp.sum(factor[:, :, None] * picked.astype(jnp.float32), axis=1)
    layer_out = (stream + expert_mix).astype(jnp.bfloat16)
    return (layer_out, device_share.reshape(1), gate_held[None], up_held[None], down_held[None])


def solution(mesh):
    in_specs = (
        P(("expert", "dp"), None),
        P(("expert", "dp"), None),
        P(("expert", "dp"), None, None),
        P(("expert", "dp"), None, None),
        P(("expert", "dp"), None),
        P(("expert", "dp"), None),
        P(("expert", "dp")),
        P(),
        P(("expert", "dp"), None),
        P(("expert", "dp"), None),
        P(),
        P(),
        P("expert", "dp", None),
        P("expert", "dp", None),
        P("expert", None, "dp"),
    )
    out_specs = (
        P(("expert", "dp"), None),
        P("expert"),
        P("expert", "dp", None),
        P("expert", "dp", None),
        P("expert", None, "dp"),
    )
    return jax.shard_map(
        per_device, mesh=mesh, in_specs=in_specs, out_specs=out_specs, check_vma=False
    )
```

```python
import jax
import jax.numpy as jnp
from jax import lax
from jax.sharding import PartitionSpec as P

QH = 32
KVH = 4
HEAD = 128


def swapped(value, axis, stride):
    mask = 2**stride
    pairs = [(source, source ^ mask) for source in range(lax.axis_size(axis))]
    return lax.ppermute(value, axis, pairs)


def attention(query_rows, key_rows, value_rows, new_key, new_value, valid_len):
    seq_count = query_rows.shape[0]
    cache_len = key_rows.shape[1]
    group = QH // KVH
    scale = HEAD ** (-0.5)
    query_view = query_rows.reshape(seq_count, KVH, group, HEAD)
    key_view = key_rows.reshape(seq_count, cache_len, KVH, HEAD)
    value_view = value_rows.reshape(seq_count, cache_len, KVH, HEAD)
    scores = (
        jnp.einsum("skgd,slkd->skgl", query_view, key_view, preferred_element_type=jnp.float32)
        * scale
    )
    valid = lax.broadcasted_iota(jnp.int32, (seq_count, cache_len), 1) < valid_len[:, None]
    scores = jnp.where(valid[:, None, None, :], scores, -1e30)
    own_score = (
        jnp.einsum(
            "skgd,skd->skg",
            query_view,
            new_key.reshape(seq_count, KVH, HEAD),
            preferred_element_type=jnp.float32,
        )
        * scale
    )
    highest = jnp.maximum(jnp.max(scores, axis=-1), own_score)
    weights = jnp.exp(scores - highest[..., None])
    own_weight = jnp.exp(own_score - highest)
    denom = jnp.sum(weights, axis=-1) + own_weight
    probs = (weights / denom[..., None]).astype(jnp.bfloat16)
    own_prob = (own_weight / denom).astype(jnp.bfloat16)
    mixed = jnp.einsum("skgl,slkd->skgd", probs, value_view, preferred_element_type=jnp.float32)
    mixed = mixed + own_prob.astype(jnp.float32)[..., None] * new_value.reshape(
        seq_count, KVH, 1, HEAD
    ).astype(jnp.float32)
    return mixed.reshape(seq_count, QH * HEAD).astype(jnp.bfloat16)


def per_device(
    skip_stream,
    attention_probes,
    stored_attention_lookups,
    stored_attention_contents,
    incoming_lookup_entries,
    incoming_content_entries,
    filled_slot_spans,
    layernorm_gain,
    routed_specialist_indices,
    routing_probabilities,
    admission_limits,
    swap_indicator,
    gating_projection_matrix,
    widening_projection_matrix,
    output_projection_matrix,
):
    experts = lax.axis_size("expert")
    groups = lax.axis_size("dp")
    half_axis = experts // 2
    far_bit = experts.bit_length() - 2
    my_index = lax.axis_index("expert")
    my_device = my_index * groups + lax.axis_index("dp")
    own_weights = (
        gating_projection_matrix[0],
        widening_projection_matrix[0],
        output_projection_matrix[0],
    )
    partner = swapped(own_weights, "expert", far_bit)
    take_other = swap_indicator[my_index] == 1
    retained_specialist = jnp.where(take_other, (my_index + half_axis) % experts, my_index)

    seq_rows = skip_stream.shape[0]
    width = skip_stream.shape[1]
    slot_cap = 2
    side_cols = 128
    expert_range = lax.broadcasted_iota(jnp.int32, (experts,), 0)

    attn = attention(
        attention_probes,
        stored_attention_lookups,
        stored_attention_contents,
        incoming_lookup_entries,
        incoming_content_entries,
        filled_slot_spans,
    )
    stream = skip_stream.astype(jnp.float32) + attn.astype(jnp.float32)
    normed = (
        stream
        * lax.rsqrt(jnp.mean(stream * stream, axis=-1, keepdims=True) + 1e-06)
        * layernorm_gain
    ).astype(jnp.bfloat16)

    route_hot = (routed_specialist_indices[:, :, None] == expert_range[None, None, :]).astype(
        jnp.int32
    )
    row_hot = jnp.sum(route_hot, axis=1)
    earlier = jnp.cumsum(row_hot, axis=0) - row_hot
    local_rank = jnp.sum(route_hot * earlier[:, None, :], axis=-1)
    slot_code = routed_specialist_indices * slot_cap + local_rank
    targets = lax.broadcasted_iota(jnp.int32, (experts * slot_cap,), 0)
    slot_hits = jnp.any(slot_code[:, :, None] == targets[None, None, :], axis=1)
    occupied = jnp.any(slot_hits, axis=0)
    row_range = lax.broadcasted_iota(jnp.int32, (seq_rows, 1), 0)
    source_row = jnp.sum(jnp.where(slot_hits, row_range, 0), axis=0) + jnp.where(
        occupied, 0, seq_rows
    )
    padded_rows = jnp.concatenate([normed, jnp.zeros((1, width), jnp.bfloat16)], axis=0)
    outgoing = padded_rows[source_row].reshape(experts, slot_cap, width)
    partner_hist = jnp.roll(jnp.sum(row_hot, axis=0), -half_axis)
    col = lax.broadcasted_iota(jnp.int32, (experts, slot_cap, side_cols), 2)
    slot_of = lax.broadcasted_iota(jnp.int32, (experts, slot_cap, side_cols), 1)
    side = jnp.where(
        col == 0,
        occupied.reshape(experts, slot_cap, 1).astype(jnp.float32),
        jnp.where(
            (col == 1) & (slot_of == 0), partner_hist[:, None, None].astype(jnp.float32), 0.0
        ),
    ).astype(jnp.bfloat16)
    payload = jnp.concatenate([outgoing, side], axis=-1)
    arrived = lax.all_to_all(payload, "expert", split_axis=0, concat_axis=0, tiled=True)
    column = lax.all_gather(arrived, "dp", axis=1, tiled=True)
    column_rows = column[:, :, :width]
    occupied_flat = column[:, :, width].astype(jnp.float32).reshape(-1)
    partner_total = jnp.sum(column[:, :, width + 1].astype(jnp.float32))
    before_count = jnp.cumsum(occupied_flat) - occupied_flat
    kept_mask = occupied_flat * (
        before_count < admission_limits[my_index].astype(jnp.float32)
    ).astype(jnp.float32)
    own_total = jnp.sum(occupied_flat)
    held_tally = jnp.where(take_other, partner_total, own_total)
    device_share = jnp.minimum(
        held_tally, admission_limits[retained_specialist].astype(jnp.float32)
    ) / (seq_rows * routed_specialist_indices.shape[1] * groups)

    gate_val = jnp.einsum(
        "esf,hf->esh", column_rows, own_weights[0], preferred_element_type=jnp.float32
    )
    up_val = jnp.einsum(
        "esf,hf->esh", column_rows, own_weights[1], preferred_element_type=jnp.float32
    )
    hidden = (jax.nn.silu(gate_val) * up_val).astype(jnp.bfloat16)
    hidden_kept = hidden * kept_mask.reshape(experts, groups * slot_cap, 1).astype(jnp.bfloat16)
    feature_cols = own_weights[2].shape[1]
    summed = jnp.einsum(
        "esn,nf->esf",
        lax.all_gather(hidden_kept, "dp", axis=2, tiled=True),
        own_weights[2],
        preferred_element_type=jnp.float32,
    )
    summed, partner = lax.optimization_barrier((summed, partner))
    results = summed.astype(jnp.bfloat16).reshape(experts, groups, slot_cap, feature_cols)
    returned = lax.all_to_all(
        lax.all_to_all(results, "expert", split_axis=0, concat_axis=0, tiled=True),
        "dp",
        split_axis=1,
        concat_axis=3,
        tiled=True,
    )
    returned_flat = returned.reshape(experts * slot_cap, width)
    picked = returned_flat[slot_code]
    expert_mix = jnp.sum(routing_probabilities[:, :, None] * picked.astype(jnp.float32), axis=1)
    layer_out = (stream + expert_mix).astype(jnp.bfloat16)
    gate_held = jnp.where(take_other, partner[0], own_weights[0])
    up_held = jnp.where(take_other, partner[1], own_weights[1])
    down_held = jnp.where(take_other, partner[2], own_weights[2])
    return (layer_out, device_share.reshape(1), gate_held[None], up_held[None], down_held[None])


def solution(mesh):
    in_specs = (
        P(("expert", "dp"), None),
        P(("expert", "dp"), None),
        P(("expert", "dp"), None, None),
        P(("expert", "dp"), None, None),
        P(("expert", "dp"), None),
        P(("expert", "dp"), None),
        P(("expert", "dp")),
        P(),
        P(("expert", "dp"), None),
        P(("expert", "dp"), None),
        P(),
        P(),
        P("expert", "dp", None),
        P("expert", "dp", None),
        P("expert", None, "dp"),
    )
    out_specs = (
        P(("expert", "dp"), None),
        P("expert"),
        P("expert", "dp", None),
        P("expert", "dp", None),
        P("expert", None, "dp"),
    )
    return jax.shard_map(
        per_device, mesh=mesh, in_specs=in_specs, out_specs=out_specs, check_vma=False
    )
```

```python
import jax
import jax.numpy as jnp
from jax import lax
from jax.sharding import PartitionSpec as P

QH = 32
KVH = 4
HEAD = 128


def swapped(value, axis, stride):
    mask = 2**stride
    pairs = [(source, source ^ mask) for source in range(lax.axis_size(axis))]
    return lax.ppermute(value, axis, pairs)


def attention(query_rows, key_rows, value_rows, new_key, new_value, valid_len):
    seq_count = query_rows.shape[0]
    cache_len = key_rows.shape[1]
    group = QH // KVH
    scale = HEAD ** (-0.5)
    query_view = query_rows.reshape(seq_count, KVH, group, HEAD)
    key_view = key_rows.reshape(seq_count, cache_len, KVH, HEAD)
    value_view = value_rows.reshape(seq_count, cache_len, KVH, HEAD)
    scores = (
        jnp.einsum("skgd,slkd->skgl", query_view, key_view, preferred_element_type=jnp.float32)
        * scale
    )
    valid = lax.broadcasted_iota(jnp.int32, (seq_count, cache_len), 1) < valid_len[:, None]
    scores = jnp.where(valid[:, None, None, :], scores, -1e30)
    own_score = (
        jnp.einsum(
            "skgd,skd->skg",
            query_view,
            new_key.reshape(seq_count, KVH, HEAD),
            preferred_element_type=jnp.float32,
        )
        * scale
    )
    highest = jnp.maximum(jnp.max(scores, axis=-1), own_score)
    weights = jnp.exp(scores - highest[..., None])
    own_weight = jnp.exp(own_score - highest)
    denom = jnp.sum(weights, axis=-1) + own_weight
    probs = (weights / denom[..., None]).astype(jnp.bfloat16)
    own_prob = (own_weight / denom).astype(jnp.bfloat16)
    mixed = jnp.einsum("skgl,slkd->skgd", probs, value_view, preferred_element_type=jnp.float32)
    mixed = mixed + own_prob.astype(jnp.float32)[..., None] * new_value.reshape(
        seq_count, KVH, 1, HEAD
    ).astype(jnp.float32)
    return mixed.reshape(seq_count, QH * HEAD).astype(jnp.bfloat16)


def per_device(
    skip_stream,
    attention_probes,
    stored_attention_lookups,
    stored_attention_contents,
    incoming_lookup_entries,
    incoming_content_entries,
    filled_slot_spans,
    layernorm_gain,
    routed_specialist_indices,
    routing_probabilities,
    admission_limits,
    swap_indicator,
    gating_projection_matrix,
    widening_projection_matrix,
    output_projection_matrix,
):
    experts = lax.axis_size("expert")
    groups = lax.axis_size("dp")
    half_axis = experts // 2
    far_bit = experts.bit_length() - 2
    my_index = lax.axis_index("expert")
    my_device = my_index * groups + lax.axis_index("dp")
    own_weights = (
        gating_projection_matrix[0],
        widening_projection_matrix[0],
        output_projection_matrix[0],
    )
    partner = swapped(own_weights, "expert", far_bit)
    take_other = swap_indicator[my_index] == 1
    retained_specialist = jnp.where(take_other, (my_index + half_axis) % experts, my_index)

    seq_rows = skip_stream.shape[0]
    width = skip_stream.shape[1]
    slot_cap = 2
    side_cols = 128
    expert_range = lax.broadcasted_iota(jnp.int32, (experts,), 0)

    attn = attention(
        attention_probes,
        stored_attention_lookups,
        stored_attention_contents,
        incoming_lookup_entries,
        incoming_content_entries,
        filled_slot_spans,
    )
    stream = skip_stream.astype(jnp.float32) + attn.astype(jnp.float32)
    normed = (
        stream
        * lax.rsqrt(jnp.mean(stream * stream, axis=-1, keepdims=True) + 1e-06)
        * layernorm_gain
    ).astype(jnp.bfloat16)

    route_hot = (routed_specialist_indices[:, :, None] == expert_range[None, None, :]).astype(
        jnp.int32
    )
    row_hot = jnp.sum(route_hot, axis=1)
    earlier = jnp.cumsum(row_hot, axis=0) - row_hot
    local_rank = jnp.sum(route_hot * earlier[:, None, :], axis=-1)
    slot_code = routed_specialist_indices * slot_cap + local_rank
    targets = lax.broadcasted_iota(jnp.int32, (experts * slot_cap,), 0)
    slot_hits = jnp.any(slot_code[:, :, None] == targets[None, None, :], axis=1)
    occupied = jnp.any(slot_hits, axis=0)
    row_range = lax.broadcasted_iota(jnp.int32, (seq_rows, 1), 0)
    source_row = jnp.sum(jnp.where(slot_hits, row_range, 0), axis=0) + jnp.where(
        occupied, 0, seq_rows
    )
    padded_rows = jnp.concatenate([normed, jnp.zeros((1, width), jnp.bfloat16)], axis=0)
    outgoing = padded_rows[source_row].reshape(experts, slot_cap, width)
    partner_hist = jnp.roll(jnp.sum(row_hot, axis=0), -half_axis)
    col = lax.broadcasted_iota(jnp.int32, (experts, slot_cap, side_cols), 2)
    slot_of = lax.broadcasted_iota(jnp.int32, (experts, slot_cap, side_cols), 1)
    side = jnp.where(
        col == 0,
        occupied.reshape(experts, slot_cap, 1).astype(jnp.float32),
        jnp.where(
            (col == 1) & (slot_of == 0), partner_hist[:, None, None].astype(jnp.float32), 0.0
        ),
    ).astype(jnp.bfloat16)
    payload = jnp.concatenate([outgoing, side], axis=-1)
    arrived = lax.all_to_all(payload, "expert", split_axis=0, concat_axis=0, tiled=True)
    column = lax.all_gather(arrived[None], "dp", axis=0, tiled=True)
    marks = column[:, :, :, width].astype(jnp.float32)
    partner_total = jnp.sum(column[:, :, :, width + 1].astype(jnp.float32))
    occupied_flat = jnp.transpose(marks, (1, 0, 2)).reshape(-1)
    before_count = jnp.cumsum(occupied_flat) - occupied_flat
    kept_flat = occupied_flat * (
        before_count < admission_limits[my_index].astype(jnp.float32)
    ).astype(jnp.float32)
    kept_mask = jnp.transpose(kept_flat.reshape(experts, groups, slot_cap), (1, 0, 2))
    own_total = jnp.sum(occupied_flat)
    held_tally = jnp.where(take_other, partner_total, own_total)
    device_share = jnp.minimum(
        held_tally, admission_limits[retained_specialist].astype(jnp.float32)
    ) / (seq_rows * routed_specialist_indices.shape[1] * groups)

    side_pad = ((0, 0), (0, side_cols))
    gate_wide = jnp.pad(own_weights[0], side_pad)
    up_wide = jnp.pad(own_weights[1], side_pad)
    gate_val = jnp.einsum(
        "desf,hf->desh", column, gate_wide, preferred_element_type=jnp.float32
    )
    up_val = jnp.einsum("desf,hf->desh", column, up_wide, preferred_element_type=jnp.float32)
    hidden = (jax.nn.silu(gate_val) * up_val).astype(jnp.bfloat16)
    hidden_kept = hidden * kept_mask[..., None].astype(jnp.bfloat16)
    unit_count = hidden_kept.shape[-1]
    hidden_all = lax.all_gather(
        hidden_kept.reshape(1, groups * experts * slot_cap, unit_count), "dp", axis=0, tiled=True
    )
    feature_cols = own_weights[2].shape[1]
    down_split = own_weights[2].reshape(groups, unit_count, feature_cols)
    summed = jnp.einsum(
        "gsn,gnf->sf", hidden_all, down_split, preferred_element_type=jnp.float32
    )
    summed, partner = lax.optimization_barrier((summed, partner))
    results = summed.astype(jnp.bfloat16).reshape(groups, experts, slot_cap, feature_cols)
    returned = lax.all_to_all(
        lax.all_to_all(results, "expert", split_axis=1, concat_axis=1, tiled=True),
        "dp",
        split_axis=0,
        concat_axis=3,
        tiled=True,
    )
    returned_flat = returned.reshape(experts * slot_cap, width)
    picked = returned_flat[slot_code]
    expert_mix = jnp.sum(routing_probabilities[:, :, None] * picked.astype(jnp.float32), axis=1)
    layer_out = (stream + expert_mix).astype(jnp.bfloat16)
    gate_held = jnp.where(take_other, partner[0], own_weights[0])
    up_held = jnp.where(take_other, partner[1], own_weights[1])
    down_held = jnp.where(take_other, partner[2], own_weights[2])
    return (layer_out, device_share.reshape(1), gate_held[None], up_held[None], down_held[None])


def solution(mesh):
    in_specs = (
        P(("expert", "dp"), None),
        P(("expert", "dp"), None),
        P(("expert", "dp"), None, None),
        P(("expert", "dp"), None, None),
        P(("expert", "dp"), None),
        P(("expert", "dp"), None),
        P(("expert", "dp")),
        P(),
        P(("expert", "dp"), None),
        P(("expert", "dp"), None),
        P(),
        P(),
        P("expert", "dp", None),
        P("expert", "dp", None),
        P("expert", None, "dp"),
    )
    out_specs = (
        P(("expert", "dp"), None),
        P("expert"),
        P("expert", "dp", None),
        P("expert", "dp", None),
        P("expert", None, "dp"),
    )
    return jax.shard_map(
        per_device, mesh=mesh, in_specs=in_specs, out_specs=out_specs, check_vma=False
    )
```

```python
import jax
import jax.numpy as jnp
from jax import lax
from jax.sharding import PartitionSpec as P

QH = 32
KVH = 4
HEAD = 128


def swapped(value, axis, stride):
    mask = 2**stride
    pairs = [(source, source ^ mask) for source in range(lax.axis_size(axis))]
    return lax.ppermute(value, axis, pairs)


def attention(query_rows, key_rows, value_rows, new_key, new_value, valid_len):
    seq_count = query_rows.shape[0]
    cache_len = key_rows.shape[1]
    group = QH // KVH
    scale = HEAD ** (-0.5)
    query_view = query_rows.reshape(seq_count, KVH, group, HEAD)
    key_view = key_rows.reshape(seq_count, cache_len, KVH, HEAD)
    value_view = value_rows.reshape(seq_count, cache_len, KVH, HEAD)
    scores = (
        jnp.einsum("skgd,slkd->skgl", query_view, key_view, preferred_element_type=jnp.float32)
        * scale
    )
    valid = lax.broadcasted_iota(jnp.int32, (seq_count, cache_len), 1) < valid_len[:, None]
    scores = jnp.where(valid[:, None, None, :], scores, -1e30)
    own_score = (
        jnp.einsum(
            "skgd,skd->skg",
            query_view,
            new_key.reshape(seq_count, KVH, HEAD),
            preferred_element_type=jnp.float32,
        )
        * scale
    )
    highest = jnp.maximum(jnp.max(scores, axis=-1), own_score)
    weights = jnp.exp(scores - highest[..., None])
    own_weight = jnp.exp(own_score - highest)
    denom = jnp.sum(weights, axis=-1) + own_weight
    probs = (weights / denom[..., None]).astype(jnp.bfloat16)
    own_prob = (own_weight / denom).astype(jnp.bfloat16)
    mixed = jnp.einsum("skgl,slkd->skgd", probs, value_view, preferred_element_type=jnp.float32)
    mixed = mixed + own_prob.astype(jnp.float32)[..., None] * new_value.reshape(
        seq_count, KVH, 1, HEAD
    ).astype(jnp.float32)
    return mixed.reshape(seq_count, QH * HEAD).astype(jnp.bfloat16)


def per_device(
    skip_stream,
    attention_probes,
    stored_attention_lookups,
    stored_attention_contents,
    incoming_lookup_entries,
    incoming_content_entries,
    filled_slot_spans,
    layernorm_gain,
    routed_specialist_indices,
    routing_probabilities,
    admission_limits,
    swap_indicator,
    gating_projection_matrix,
    widening_projection_matrix,
    output_projection_matrix,
):
    experts = lax.axis_size("expert")
    groups = lax.axis_size("dp")
    half_axis = experts // 2
    far_bit = experts.bit_length() - 2
    my_index = lax.axis_index("expert")
    my_device = my_index * groups + lax.axis_index("dp")
    own_weights = (
        gating_projection_matrix[0],
        widening_projection_matrix[0],
        output_projection_matrix[0],
    )
    partner = swapped(own_weights, "expert", far_bit)
    take_other = swap_indicator[my_index] == 1
    retained_specialist = jnp.where(take_other, (my_index + half_axis) % experts, my_index)

    seq_rows = skip_stream.shape[0]
    width = skip_stream.shape[1]
    slot_cap = 2
    side_cols = 128
    expert_range = lax.broadcasted_iota(jnp.int32, (experts,), 0)

    attn = attention(
        attention_probes,
        stored_attention_lookups,
        stored_attention_contents,
        incoming_lookup_entries,
        incoming_content_entries,
        filled_slot_spans,
    )
    stream = skip_stream.astype(jnp.float32) + attn.astype(jnp.float32)
    normed = (
        stream
        * lax.rsqrt(jnp.mean(stream * stream, axis=-1, keepdims=True) + 1e-06)
        * layernorm_gain
    ).astype(jnp.bfloat16)

    route_hot = (routed_specialist_indices[:, :, None] == expert_range[None, None, :]).astype(
        jnp.int32
    )
    row_hot = jnp.sum(route_hot, axis=1)
    earlier = jnp.cumsum(row_hot, axis=0) - row_hot
    local_rank = jnp.sum(route_hot * earlier[:, None, :], axis=-1)
    slot_code = routed_specialist_indices * slot_cap + local_rank
    targets = lax.broadcasted_iota(jnp.int32, (experts * slot_cap,), 0)
    slot_hits = jnp.any(slot_code[:, :, None] == targets[None, None, :], axis=1)
    occupied = jnp.any(slot_hits, axis=0)
    row_range = lax.broadcasted_iota(jnp.int32, (seq_rows, 1), 0)
    source_row = jnp.sum(jnp.where(slot_hits, row_range, 0), axis=0) + jnp.where(
        occupied, 0, seq_rows
    )
    padded_rows = jnp.concatenate([normed, jnp.zeros((1, width), jnp.bfloat16)], axis=0)
    outgoing = padded_rows[source_row].reshape(experts, slot_cap, width)
    partner_hist = jnp.roll(jnp.sum(row_hot, axis=0), -half_axis)
    col = lax.broadcasted_iota(jnp.int32, (experts, slot_cap, side_cols), 2)
    slot_of = lax.broadcasted_iota(jnp.int32, (experts, slot_cap, side_cols), 1)
    side = jnp.where(
        col == 0,
        occupied.reshape(experts, slot_cap, 1).astype(jnp.float32),
        jnp.where(
            (col == 1) & (slot_of == 0), partner_hist[:, None, None].astype(jnp.float32), 0.0
        ),
    ).astype(jnp.bfloat16)
    payload = jnp.concatenate([outgoing, side], axis=-1)
    side_pad = ((0, 0), (0, side_cols))
    gate_wide = jnp.pad(own_weights[0], side_pad)
    up_wide = jnp.pad(own_weights[1], side_pad)
    feature_cols = own_weights[2].shape[1]
    unit_count = own_weights[0].shape[0]
    down_split = own_weights[2].reshape(groups, unit_count, feature_cols)
    columns = []
    for chunk in range(slot_cap):
        arrived = lax.all_to_all(
            payload[:, chunk], "expert", split_axis=0, concat_axis=0, tiled=True
        )
        columns.append(lax.all_gather(arrived[None], "dp", axis=0, tiled=True))
    marks = jnp.stack([c[:, :, width] for c in columns], axis=-1).astype(jnp.float32)
    partner_total = sum(jnp.sum(c[:, :, width + 1].astype(jnp.float32)) for c in columns)
    occupied_flat = jnp.transpose(marks, (1, 0, 2)).reshape(-1)
    before_count = jnp.cumsum(occupied_flat) - occupied_flat
    kept_flat = occupied_flat * (
        before_count < admission_limits[my_index].astype(jnp.float32)
    ).astype(jnp.float32)
    kept_mask = jnp.transpose(kept_flat.reshape(experts, groups, slot_cap), (1, 0, 2))
    own_total = jnp.sum(occupied_flat)
    held_tally = jnp.where(take_other, partner_total, own_total)
    device_share = jnp.minimum(
        held_tally, admission_limits[retained_specialist].astype(jnp.float32)
    ) / (seq_rows * routed_specialist_indices.shape[1] * groups)

    returned_parts = []
    for chunk in range(slot_cap):
        column = columns[chunk]
        gate_val = jnp.einsum(
            "def,hf->deh", column, gate_wide, preferred_element_type=jnp.float32
        )
        up_val = jnp.einsum("def,hf->deh", column, up_wide, preferred_element_type=jnp.float32)
        hidden = (jax.nn.silu(gate_val) * up_val).astype(jnp.bfloat16)
        hidden_all = lax.all_gather(
            hidden.reshape(1, groups * experts, unit_count), "dp", axis=0, tiled=True
        )
        summed = jnp.einsum(
            "gsn,gnf->sf", hidden_all, down_split, preferred_element_type=jnp.float32
        )
        if chunk == slot_cap - 1:
            summed, partner = lax.optimization_barrier((summed, partner))
        results = summed.astype(jnp.bfloat16).reshape(groups, experts, feature_cols)
        results = results * kept_mask[:, :, chunk, None].astype(jnp.bfloat16)
        returned_parts.append(
            lax.all_to_all(
                lax.all_to_all(results, "expert", split_axis=1, concat_axis=1, tiled=True),
                "dp",
                split_axis=0,
                concat_axis=2,
                tiled=True,
            )
        )
    returned = jnp.stack([r[0] for r in returned_parts], axis=1)
    returned_flat = returned.reshape(experts * slot_cap, width)
    picked = returned_flat[slot_code]
    expert_mix = jnp.sum(routing_probabilities[:, :, None] * picked.astype(jnp.float32), axis=1)
    layer_out = (stream + expert_mix).astype(jnp.bfloat16)
    gate_held = jnp.where(take_other, partner[0], own_weights[0])
    up_held = jnp.where(take_other, partner[1], own_weights[1])
    down_held = jnp.where(take_other, partner[2], own_weights[2])
    return (layer_out, device_share.reshape(1), gate_held[None], up_held[None], down_held[None])


def solution(mesh):
    in_specs = (
        P(("expert", "dp"), None),
        P(("expert", "dp"), None),
        P(("expert", "dp"), None, None),
        P(("expert", "dp"), None, None),
        P(("expert", "dp"), None),
        P(("expert", "dp"), None),
        P(("expert", "dp")),
        P(),
        P(("expert", "dp"), None),
        P(("expert", "dp"), None),
        P(),
        P(),
        P("expert", "dp", None),
        P("expert", "dp", None),
        P("expert", None, "dp"),
    )
    out_specs = (
        P(("expert", "dp"), None),
        P("expert"),
        P("expert", "dp", None),
        P("expert", "dp", None),
        P("expert", None, "dp"),
    )
    return jax.shard_map(
        per_device, mesh=mesh, in_specs=in_specs, out_specs=out_specs, check_vma=False
    )
```

```python
import jax
import jax.numpy as jnp
from jax import lax
from jax.sharding import PartitionSpec as P

QH = 32
KVH = 4
HEAD = 128


def swapped(value, axis, stride):
    mask = 2**stride
    pairs = [(source, source ^ mask) for source in range(lax.axis_size(axis))]
    return lax.ppermute(value, axis, pairs)


def attention(query_rows, key_rows, value_rows, new_key, new_value, valid_len):
    seq_count = query_rows.shape[0]
    cache_len = key_rows.shape[1]
    group = QH // KVH
    scale = HEAD ** (-0.5)
    query_view = query_rows.reshape(seq_count, KVH, group, HEAD)
    key_view = key_rows.reshape(seq_count, cache_len, KVH, HEAD)
    value_view = value_rows.reshape(seq_count, cache_len, KVH, HEAD)
    scores = (
        jnp.einsum("skgd,slkd->skgl", query_view, key_view, preferred_element_type=jnp.float32)
        * scale
    )
    valid = lax.broadcasted_iota(jnp.int32, (seq_count, cache_len), 1) < valid_len[:, None]
    scores = jnp.where(valid[:, None, None, :], scores, -1e30)
    own_score = (
        jnp.einsum(
            "skgd,skd->skg",
            query_view,
            new_key.reshape(seq_count, KVH, HEAD),
            preferred_element_type=jnp.float32,
        )
        * scale
    )
    highest = jnp.maximum(jnp.max(scores, axis=-1), own_score)
    weights = jnp.exp(scores - highest[..., None])
    own_weight = jnp.exp(own_score - highest)
    denom = jnp.sum(weights, axis=-1) + own_weight
    probs = (weights / denom[..., None]).astype(jnp.bfloat16)
    own_prob = (own_weight / denom).astype(jnp.bfloat16)
    mixed = jnp.einsum("skgl,slkd->skgd", probs, value_view, preferred_element_type=jnp.float32)
    mixed = mixed + own_prob.astype(jnp.float32)[..., None] * new_value.reshape(
        seq_count, KVH, 1, HEAD
    ).astype(jnp.float32)
    return mixed.reshape(seq_count, QH * HEAD).astype(jnp.bfloat16)


def per_device(
    skip_stream,
    attention_probes,
    stored_attention_lookups,
    stored_attention_contents,
    incoming_lookup_entries,
    incoming_content_entries,
    filled_slot_spans,
    layernorm_gain,
    routed_specialist_indices,
    routing_probabilities,
    admission_limits,
    swap_indicator,
    gating_projection_matrix,
    widening_projection_matrix,
    output_projection_matrix,
):
    experts = lax.axis_size("expert")
    groups = lax.axis_size("dp")
    half_axis = experts // 2
    far_bit = experts.bit_length() - 2
    my_index = lax.axis_index("expert")
    my_device = my_index * groups + lax.axis_index("dp")
    own_weights = (
        gating_projection_matrix[0],
        widening_projection_matrix[0],
        output_projection_matrix[0],
    )
    partner = swapped(own_weights, "expert", far_bit)
    take_other = swap_indicator[my_index] == 1
    retained_specialist = jnp.where(take_other, (my_index + half_axis) % experts, my_index)

    seq_rows = skip_stream.shape[0]
    width = skip_stream.shape[1]
    slot_cap = 2
    side_cols = 128
    expert_range = lax.broadcasted_iota(jnp.int32, (experts,), 0)

    attn = attention(
        attention_probes,
        stored_attention_lookups,
        stored_attention_contents,
        incoming_lookup_entries,
        incoming_content_entries,
        filled_slot_spans,
    )
    stream = skip_stream.astype(jnp.float32) + attn.astype(jnp.float32)
    normed = (
        stream
        * lax.rsqrt(jnp.mean(stream * stream, axis=-1, keepdims=True) + 1e-06)
        * layernorm_gain
    ).astype(jnp.bfloat16)

    route_hot = (routed_specialist_indices[:, :, None] == expert_range[None, None, :]).astype(
        jnp.int32
    )
    row_hot = jnp.sum(route_hot, axis=1)
    earlier = jnp.cumsum(row_hot, axis=0) - row_hot
    local_rank = jnp.sum(route_hot * earlier[:, None, :], axis=-1)
    slot_code = routed_specialist_indices * slot_cap + local_rank
    targets = lax.broadcasted_iota(jnp.int32, (experts * slot_cap,), 0)
    slot_hits = jnp.any(slot_code[:, :, None] == targets[None, None, :], axis=1)
    occupied = jnp.any(slot_hits, axis=0)
    row_range = lax.broadcasted_iota(jnp.int32, (seq_rows, 1), 0)
    source_row = jnp.sum(jnp.where(slot_hits, row_range, 0), axis=0) + jnp.where(
        occupied, 0, seq_rows
    )
    padded_rows = jnp.concatenate([normed, jnp.zeros((1, width), jnp.bfloat16)], axis=0)
    outgoing = padded_rows[source_row].reshape(experts, slot_cap, width)
    partner_hist = jnp.roll(jnp.sum(row_hot, axis=0), -half_axis)
    col = lax.broadcasted_iota(jnp.int32, (experts, slot_cap, side_cols), 2)
    slot_of = lax.broadcasted_iota(jnp.int32, (experts, slot_cap, side_cols), 1)
    side = jnp.where(
        col == 0,
        occupied.reshape(experts, slot_cap, 1).astype(jnp.float32),
        jnp.where(
            (col == 1) & (slot_of == 0), partner_hist[:, None, None].astype(jnp.float32), 0.0
        ),
    ).astype(jnp.bfloat16)
    payload = jnp.concatenate([outgoing, side], axis=-1)
    arrived = lax.all_to_all(payload, "expert", split_axis=0, concat_axis=0, tiled=True)
    column = lax.all_gather(arrived[None], "dp", axis=0, tiled=True)
    marks = column[:, :, :, width].astype(jnp.float32)
    partner_total = jnp.sum(column[:, :, :, width + 1].astype(jnp.float32))
    occupied_flat = jnp.transpose(marks, (1, 0, 2)).reshape(-1)
    before_count = jnp.cumsum(occupied_flat) - occupied_flat
    kept_flat = occupied_flat * (
        before_count < admission_limits[my_index].astype(jnp.float32)
    ).astype(jnp.float32)
    kept_mask = jnp.transpose(kept_flat.reshape(experts, groups, slot_cap), (1, 0, 2))
    own_total = jnp.sum(occupied_flat)
    held_tally = jnp.where(take_other, partner_total, own_total)
    device_share = jnp.minimum(
        held_tally, admission_limits[retained_specialist].astype(jnp.float32)
    ) / (seq_rows * routed_specialist_indices.shape[1] * groups)

    side_pad = ((0, 0), (0, side_cols))
    gate_wide = jnp.pad(own_weights[0], side_pad)
    up_wide = jnp.pad(own_weights[1], side_pad)
    gate_val = jnp.einsum(
        "desf,hf->desh", column, gate_wide, preferred_element_type=jnp.float32
    )
    up_val = jnp.einsum("desf,hf->desh", column, up_wide, preferred_element_type=jnp.float32)
    hidden = (jax.nn.silu(gate_val) * up_val).astype(jnp.bfloat16)
    hidden_kept = hidden * kept_mask[..., None].astype(jnp.bfloat16)
    unit_count = hidden_kept.shape[-1]
    hidden_all = lax.all_gather(
        hidden_kept.reshape(1, groups * experts * slot_cap, unit_count), "dp", axis=0, tiled=True
    )
    feature_cols = own_weights[2].shape[1]
    down_split = own_weights[2].reshape(groups, unit_count, feature_cols)
    summed = jnp.einsum(
        "gsn,gnf->sf", hidden_all, down_split, preferred_element_type=jnp.float32
    )
    results = summed.astype(jnp.bfloat16).reshape(groups, experts, slot_cap, feature_cols)
    returned = lax.all_to_all(
        lax.all_to_all(results, "expert", split_axis=1, concat_axis=1, tiled=True),
        "dp",
        split_axis=0,
        concat_axis=3,
        tiled=True,
    )
    returned_flat = returned.reshape(experts * slot_cap, width)
    picked = returned_flat[slot_code]
    expert_mix = jnp.sum(routing_probabilities[:, :, None] * picked.astype(jnp.float32), axis=1)
    layer_out = (stream + expert_mix).astype(jnp.bfloat16)
    gate_held = jnp.where(take_other, partner[0], own_weights[0])
    up_held = jnp.where(take_other, partner[1], own_weights[1])
    down_held = jnp.where(take_other, partner[2], own_weights[2])
    return (layer_out, device_share.reshape(1), gate_held[None], up_held[None], down_held[None])


def solution(mesh):
    in_specs = (
        P(("expert", "dp"), None),
        P(("expert", "dp"), None),
        P(("expert", "dp"), None, None),
        P(("expert", "dp"), None, None),
        P(("expert", "dp"), None),
        P(("expert", "dp"), None),
        P(("expert", "dp")),
        P(),
        P(("expert", "dp"), None),
        P(("expert", "dp"), None),
        P(),
        P(),
        P("expert", "dp", None),
        P("expert", "dp", None),
        P("expert", None, "dp"),
    )
    out_specs = (
        P(("expert", "dp"), None),
        P("expert"),
        P("expert", "dp", None),
        P("expert", "dp", None),
        P("expert", None, "dp"),
    )
    return jax.shard_map(
        per_device, mesh=mesh, in_specs=in_specs, out_specs=out_specs, check_vma=False
    )
```

```python
import jax
import jax.numpy as jnp
from jax import lax
from jax.sharding import PartitionSpec as P

QH = 32
KVH = 4
HEAD = 128


def swapped(value, axis, stride):
    mask = 2**stride
    pairs = [(source, source ^ mask) for source in range(lax.axis_size(axis))]
    return lax.ppermute(value, axis, pairs)


def attention(query_rows, key_rows, value_rows, new_key, new_value, valid_len):
    seq_count = query_rows.shape[0]
    cache_len = key_rows.shape[1]
    group = QH // KVH
    scale = HEAD ** (-0.5)
    query_view = query_rows.reshape(seq_count, KVH, group, HEAD)
    key_view = key_rows.reshape(seq_count, cache_len, KVH, HEAD)
    value_view = value_rows.reshape(seq_count, cache_len, KVH, HEAD)
    scores = (
        jnp.einsum("skgd,slkd->skgl", query_view, key_view, preferred_element_type=jnp.float32)
        * scale
    )
    valid = lax.broadcasted_iota(jnp.int32, (seq_count, cache_len), 1) < valid_len[:, None]
    scores = jnp.where(valid[:, None, None, :], scores, -1e30)
    own_score = (
        jnp.einsum(
            "skgd,skd->skg",
            query_view,
            new_key.reshape(seq_count, KVH, HEAD),
            preferred_element_type=jnp.float32,
        )
        * scale
    )
    highest = jnp.maximum(jnp.max(scores, axis=-1), own_score)
    weights = jnp.exp(scores - highest[..., None])
    own_weight = jnp.exp(own_score - highest)
    denom = jnp.sum(weights, axis=-1) + own_weight
    probs = (weights / denom[..., None]).astype(jnp.bfloat16)
    own_prob = (own_weight / denom).astype(jnp.bfloat16)
    mixed = jnp.einsum("skgl,slkd->skgd", probs, value_view, preferred_element_type=jnp.float32)
    mixed = mixed + own_prob.astype(jnp.float32)[..., None] * new_value.reshape(
        seq_count, KVH, 1, HEAD
    ).astype(jnp.float32)
    return mixed.reshape(seq_count, QH * HEAD).astype(jnp.bfloat16)


def per_device(
    skip_stream,
    attention_probes,
    stored_attention_lookups,
    stored_attention_contents,
    incoming_lookup_entries,
    incoming_content_entries,
    filled_slot_spans,
    layernorm_gain,
    routed_specialist_indices,
    routing_probabilities,
    admission_limits,
    swap_indicator,
    gating_projection_matrix,
    widening_projection_matrix,
    output_projection_matrix,
):
    experts = lax.axis_size("expert")
    groups = lax.axis_size("dp")
    half_axis = experts // 2
    far_bit = experts.bit_length() - 2
    my_index = lax.axis_index("expert")
    my_device = my_index * groups + lax.axis_index("dp")
    own_weights = (
        gating_projection_matrix[0],
        widening_projection_matrix[0],
        output_projection_matrix[0],
    )
    partner = swapped(own_weights, "expert", far_bit)
    take_other = swap_indicator[my_index] == 1
    retained_specialist = jnp.where(take_other, (my_index + half_axis) % experts, my_index)

    seq_rows = skip_stream.shape[0]
    width = skip_stream.shape[1]
    slot_cap = 2
    side_cols = 128
    expert_range = lax.broadcasted_iota(jnp.int32, (experts,), 0)

    attn = attention(
        attention_probes,
        stored_attention_lookups,
        stored_attention_contents,
        incoming_lookup_entries,
        incoming_content_entries,
        filled_slot_spans,
    )
    stream = skip_stream.astype(jnp.float32) + attn.astype(jnp.float32)
    normed = (
        stream
        * lax.rsqrt(jnp.mean(stream * stream, axis=-1, keepdims=True) + 1e-06)
        * layernorm_gain
    ).astype(jnp.bfloat16)

    route_hot = (routed_specialist_indices[:, :, None] == expert_range[None, None, :]).astype(
        jnp.int32
    )
    row_hot = jnp.sum(route_hot, axis=1)
    earlier = jnp.cumsum(row_hot, axis=0) - row_hot
    local_rank = jnp.sum(route_hot * earlier[:, None, :], axis=-1)
    slot_code = routed_specialist_indices * slot_cap + local_rank
    targets = lax.broadcasted_iota(jnp.int32, (experts * slot_cap,), 0)
    slot_hits = jnp.any(slot_code[:, :, None] == targets[None, None, :], axis=1)
    occupied = jnp.any(slot_hits, axis=0)
    row_range = lax.broadcasted_iota(jnp.int32, (seq_rows, 1), 0)
    source_row = jnp.sum(jnp.where(slot_hits, row_range, 0), axis=0) + jnp.where(
        occupied, 0, seq_rows
    )
    padded_rows = jnp.concatenate([normed, jnp.zeros((1, width), jnp.bfloat16)], axis=0)
    outgoing = padded_rows[source_row].reshape(experts, slot_cap, width)
    partner_hist = jnp.roll(jnp.sum(row_hot, axis=0), -half_axis)
    col = lax.broadcasted_iota(jnp.int32, (experts, slot_cap, side_cols), 2)
    slot_of = lax.broadcasted_iota(jnp.int32, (experts, slot_cap, side_cols), 1)
    side = jnp.where(
        col == 0,
        occupied.reshape(experts, slot_cap, 1).astype(jnp.float32),
        jnp.where(
            (col == 1) & (slot_of == 0), partner_hist[:, None, None].astype(jnp.float32), 0.0
        ),
    ).astype(jnp.bfloat16)
    payload = jnp.concatenate([outgoing, side], axis=-1)
    side_pad = ((0, 0), (0, side_cols))
    gate_full = lax.all_gather(jnp.pad(own_weights[0], side_pad), "dp", axis=0, tiled=True)
    up_full = lax.all_gather(jnp.pad(own_weights[1], side_pad), "dp", axis=0, tiled=True)
    down_full = lax.all_gather(own_weights[2][None], "dp", axis=0, tiled=True)

    arrived = lax.all_to_all(payload, "expert", split_axis=0, concat_axis=0, tiled=True)
    side_all = lax.all_gather(arrived[None, :, :, width:width + 2], "dp", axis=0, tiled=True)
    marks = side_all[..., 0].astype(jnp.float32)
    partner_total = jnp.sum(side_all[..., 1].astype(jnp.float32))
    occupied_flat = jnp.transpose(marks, (1, 0, 2)).reshape(-1)
    before_count = jnp.cumsum(occupied_flat) - occupied_flat
    kept_flat = occupied_flat * (
        before_count < admission_limits[my_index].astype(jnp.float32)
    ).astype(jnp.float32)
    kept_mine = kept_flat.reshape(experts, groups, slot_cap)[:, lax.axis_index("dp")]
    own_total = jnp.sum(occupied_flat)
    held_tally = jnp.where(take_other, partner_total, own_total)
    device_share = jnp.minimum(
        held_tally, admission_limits[retained_specialist].astype(jnp.float32)
    ) / (seq_rows * routed_specialist_indices.shape[1] * groups)

    gate_val = jnp.einsum("esf,hf->esh", arrived, gate_full, preferred_element_type=jnp.float32)
    up_val = jnp.einsum("esf,hf->esh", arrived, up_full, preferred_element_type=jnp.float32)
    hidden = (jax.nn.silu(gate_val) * up_val).astype(jnp.bfloat16)
    summed = jnp.einsum("esn,gnf->esgf", hidden, down_full, preferred_element_type=jnp.float32)
    results = summed.reshape(experts, slot_cap, width).astype(jnp.bfloat16)
    results = results * kept_mine[..., None].astype(jnp.bfloat16)
    returned = lax.all_to_all(results, "expert", split_axis=0, concat_axis=0, tiled=True)
    returned_flat = returned.reshape(experts * slot_cap, width)
    picked = returned_flat[slot_code]
    expert_mix = jnp.sum(routing_probabilities[:, :, None] * picked.astype(jnp.float32), axis=1)
    layer_out = (stream + expert_mix).astype(jnp.bfloat16)
    gate_held = jnp.where(take_other, partner[0], own_weights[0])
    up_held = jnp.where(take_other, partner[1], own_weights[1])
    down_held = jnp.where(take_other, partner[2], own_weights[2])
    return (layer_out, device_share.reshape(1), gate_held[None], up_held[None], down_held[None])


def solution(mesh):
    in_specs = (
        P(("expert", "dp"), None),
        P(("expert", "dp"), None),
        P(("expert", "dp"), None, None),
        P(("expert", "dp"), None, None),
        P(("expert", "dp"), None),
        P(("expert", "dp"), None),
        P(("expert", "dp")),
        P(),
        P(("expert", "dp"), None),
        P(("expert", "dp"), None),
        P(),
        P(),
        P("expert", "dp", None),
        P("expert", "dp", None),
        P("expert", None, "dp"),
    )
    out_specs = (
        P(("expert", "dp"), None),
        P("expert"),
        P("expert", "dp", None),
        P("expert", "dp", None),
        P("expert", None, "dp"),
    )
    return jax.shard_map(
        per_device, mesh=mesh, in_specs=in_specs, out_specs=out_specs, check_vma=False
    )
```

```python
import jax
import jax.numpy as jnp
from jax import lax
from jax.sharding import PartitionSpec as P

QH = 32
KVH = 4
HEAD = 128


def swapped(value, axis, stride):
    mask = 2**stride
    pairs = [(source, source ^ mask) for source in range(lax.axis_size(axis))]
    return lax.ppermute(value, axis, pairs)


def attention(query_rows, key_rows, value_rows, new_key, new_value, valid_len):
    seq_count = query_rows.shape[0]
    cache_len = key_rows.shape[1]
    group = QH // KVH
    scale = HEAD ** (-0.5)
    query_view = query_rows.reshape(seq_count, KVH, group, HEAD)
    key_view = key_rows.reshape(seq_count, cache_len, KVH, HEAD)
    value_view = value_rows.reshape(seq_count, cache_len, KVH, HEAD)
    scores = (
        jnp.einsum("skgd,slkd->skgl", query_view, key_view, preferred_element_type=jnp.float32)
        * scale
    )
    valid = lax.broadcasted_iota(jnp.int32, (seq_count, cache_len), 1) < valid_len[:, None]
    scores = jnp.where(valid[:, None, None, :], scores, -1e30)
    own_score = (
        jnp.einsum(
            "skgd,skd->skg",
            query_view,
            new_key.reshape(seq_count, KVH, HEAD),
            preferred_element_type=jnp.float32,
        )
        * scale
    )
    highest = jnp.maximum(jnp.max(scores, axis=-1), own_score)
    weights = jnp.exp(scores - highest[..., None])
    own_weight = jnp.exp(own_score - highest)
    denom = jnp.sum(weights, axis=-1) + own_weight
    probs = (weights / denom[..., None]).astype(jnp.bfloat16)
    own_prob = (own_weight / denom).astype(jnp.bfloat16)
    mixed = jnp.einsum("skgl,slkd->skgd", probs, value_view, preferred_element_type=jnp.float32)
    mixed = mixed + own_prob.astype(jnp.float32)[..., None] * new_value.reshape(
        seq_count, KVH, 1, HEAD
    ).astype(jnp.float32)
    return mixed.reshape(seq_count, QH * HEAD).astype(jnp.bfloat16)


def per_device(
    skip_stream,
    attention_probes,
    stored_attention_lookups,
    stored_attention_contents,
    incoming_lookup_entries,
    incoming_content_entries,
    filled_slot_spans,
    layernorm_gain,
    routed_specialist_indices,
    routing_probabilities,
    admission_limits,
    swap_indicator,
    gating_projection_matrix,
    widening_projection_matrix,
    output_projection_matrix,
):
    experts = lax.axis_size("expert")
    groups = lax.axis_size("dp")
    half_axis = experts // 2
    far_bit = experts.bit_length() - 2
    my_index = lax.axis_index("expert")
    my_device = my_index * groups + lax.axis_index("dp")
    own_weights = (
        gating_projection_matrix[0],
        widening_projection_matrix[0],
        output_projection_matrix[0],
    )
    partner = swapped(own_weights, "expert", far_bit)
    take_other = swap_indicator[my_index] == 1
    retained_specialist = jnp.where(take_other, (my_index + half_axis) % experts, my_index)

    seq_rows = skip_stream.shape[0]
    width = skip_stream.shape[1]
    slot_cap = 2
    side_cols = 128
    expert_range = lax.broadcasted_iota(jnp.int32, (experts,), 0)

    attn = attention(
        attention_probes,
        stored_attention_lookups,
        stored_attention_contents,
        incoming_lookup_entries,
        incoming_content_entries,
        filled_slot_spans,
    )
    stream = skip_stream.astype(jnp.float32) + attn.astype(jnp.float32)
    normed = (
        stream
        * lax.rsqrt(jnp.mean(stream * stream, axis=-1, keepdims=True) + 1e-06)
        * layernorm_gain
    ).astype(jnp.bfloat16)

    route_hot = (routed_specialist_indices[:, :, None] == expert_range[None, None, :]).astype(
        jnp.int32
    )
    row_hot = jnp.sum(route_hot, axis=1)
    earlier = jnp.cumsum(row_hot, axis=0) - row_hot
    local_rank = jnp.sum(route_hot * earlier[:, None, :], axis=-1)
    slot_code = routed_specialist_indices * slot_cap + local_rank
    targets = lax.broadcasted_iota(jnp.int32, (experts * slot_cap,), 0)
    slot_hits = jnp.any(slot_code[:, :, None] == targets[None, None, :], axis=1)
    occupied = jnp.any(slot_hits, axis=0)
    row_range = lax.broadcasted_iota(jnp.int32, (seq_rows, 1), 0)
    source_row = jnp.sum(jnp.where(slot_hits, row_range, 0), axis=0) + jnp.where(
        occupied, 0, seq_rows
    )
    padded_rows = jnp.concatenate([normed, jnp.zeros((1, width), jnp.bfloat16)], axis=0)
    outgoing = padded_rows[source_row].reshape(experts, slot_cap, width)
    partner_hist = jnp.roll(jnp.sum(row_hot, axis=0), -half_axis)
    col = lax.broadcasted_iota(jnp.int32, (experts, slot_cap, side_cols), 2)
    slot_of = lax.broadcasted_iota(jnp.int32, (experts, slot_cap, side_cols), 1)
    side = jnp.where(
        col == 0,
        occupied.reshape(experts, slot_cap, 1).astype(jnp.float32),
        jnp.where(
            (col == 1) & (slot_of == 0), partner_hist[:, None, None].astype(jnp.float32), 0.0
        ),
    ).astype(jnp.bfloat16)
    payload = jnp.concatenate([outgoing, side], axis=-1)
    arrived = lax.all_to_all(payload, "expert", split_axis=0, concat_axis=0, tiled=True)
    column = lax.all_gather(arrived[None], "dp", axis=0, tiled=True)
    marks = column[:, :, :, width].astype(jnp.float32)
    partner_total = jnp.sum(column[:, :, :, width + 1].astype(jnp.float32))
    occupied_flat = jnp.transpose(marks, (1, 0, 2)).reshape(-1)
    before_count = jnp.cumsum(occupied_flat) - occupied_flat
    kept_flat = occupied_flat * (
        before_count < admission_limits[my_index].astype(jnp.float32)
    ).astype(jnp.float32)
    kept_mask = jnp.transpose(kept_flat.reshape(experts, groups, slot_cap), (1, 0, 2))
    own_total = jnp.sum(occupied_flat)
    held_tally = jnp.where(take_other, partner_total, own_total)
    device_share = jnp.minimum(
        held_tally, admission_limits[retained_specialist].astype(jnp.float32)
    ) / (seq_rows * routed_specialist_indices.shape[1] * groups)

    side_pad = ((0, 0), (0, side_cols))
    gate_wide = jnp.pad(own_weights[0], side_pad)
    up_wide = jnp.pad(own_weights[1], side_pad)
    gate_val = jnp.einsum(
        "desf,hf->desh", column, gate_wide, preferred_element_type=jnp.float32
    )
    up_val = jnp.einsum("desf,hf->desh", column, up_wide, preferred_element_type=jnp.float32)
    hidden = (jax.nn.silu(gate_val) * up_val).astype(jnp.bfloat16)
    hidden_kept = hidden * kept_mask[..., None].astype(jnp.bfloat16)
    unit_count = hidden_kept.shape[-1]
    hidden_col = lax.all_to_all(hidden_kept, "dp", split_axis=0, concat_axis=3, tiled=True)[0]
    own_down = own_weights[2]
    down_blocks = [own_down] + [
        lax.ppermute(own_down, "dp", [(j, (j + k) % groups) for j in range(groups)])
        for k in range(1, groups)
    ]
    down_shifted = jnp.stack(down_blocks, axis=0)
    summed = jnp.einsum(
        "esn,knf->eskf", hidden_col, down_shifted, preferred_element_type=jnp.float32
    )
    block_of = (lax.axis_index("dp") - lax.broadcasted_iota(jnp.int32, (groups,), 0)) % groups
    summed = jnp.take(summed.astype(jnp.bfloat16), block_of, axis=2)
    results = summed.reshape(experts, slot_cap, width)
    returned = lax.all_to_all(results, "expert", split_axis=0, concat_axis=0, tiled=True)
    returned_flat = returned.reshape(experts * slot_cap, width)
    picked = returned_flat[slot_code]
    expert_mix = jnp.sum(routing_probabilities[:, :, None] * picked.astype(jnp.float32), axis=1)
    layer_out = (stream + expert_mix).astype(jnp.bfloat16)
    gate_held = jnp.where(take_other, partner[0], own_weights[0])
    up_held = jnp.where(take_other, partner[1], own_weights[1])
    down_held = jnp.where(take_other, partner[2], own_weights[2])
    return (layer_out, device_share.reshape(1), gate_held[None], up_held[None], down_held[None])


def solution(mesh):
    in_specs = (
        P(("expert", "dp"), None),
        P(("expert", "dp"), None),
        P(("expert", "dp"), None, None),
        P(("expert", "dp"), None, None),
        P(("expert", "dp"), None),
        P(("expert", "dp"), None),
        P(("expert", "dp")),
        P(),
        P(("expert", "dp"), None),
        P(("expert", "dp"), None),
        P(),
        P(),
        P("expert", "dp", None),
        P("expert", "dp", None),
        P("expert", None, "dp"),
    )
    out_specs = (
        P(("expert", "dp"), None),
        P("expert"),
        P("expert", "dp", None),
        P("expert", "dp", None),
        P("expert", None, "dp"),
    )
    return jax.shard_map(
        per_device, mesh=mesh, in_specs=in_specs, out_specs=out_specs, check_vma=False
    )
```

```python
import jax
import jax.numpy as jnp
from jax import lax
from jax.sharding import PartitionSpec as P

QH = 32
KVH = 4
HEAD = 128


def swapped(value, axis, stride):
    mask = 2**stride
    pairs = [(source, source ^ mask) for source in range(lax.axis_size(axis))]
    return lax.ppermute(value, axis, pairs)


def attention(query_rows, key_rows, value_rows, new_key, new_value, valid_len):
    seq_count = query_rows.shape[0]
    cache_len = key_rows.shape[1]
    group = QH // KVH
    scale = HEAD ** (-0.5)
    query_view = query_rows.reshape(seq_count, KVH, group, HEAD)
    key_view = key_rows.reshape(seq_count, cache_len, KVH, HEAD)
    value_view = value_rows.reshape(seq_count, cache_len, KVH, HEAD)
    scores = (
        jnp.einsum("skgd,slkd->skgl", query_view, key_view, preferred_element_type=jnp.float32)
        * scale
    )
    valid = lax.broadcasted_iota(jnp.int32, (seq_count, cache_len), 1) < valid_len[:, None]
    scores = jnp.where(valid[:, None, None, :], scores, -1e30)
    own_score = (
        jnp.einsum(
            "skgd,skd->skg",
            query_view,
            new_key.reshape(seq_count, KVH, HEAD),
            preferred_element_type=jnp.float32,
        )
        * scale
    )
    highest = jnp.maximum(jnp.max(scores, axis=-1), own_score)
    weights = jnp.exp(scores - highest[..., None])
    own_weight = jnp.exp(own_score - highest)
    denom = jnp.sum(weights, axis=-1) + own_weight
    probs = (weights / denom[..., None]).astype(jnp.bfloat16)
    own_prob = (own_weight / denom).astype(jnp.bfloat16)
    mixed = jnp.einsum("skgl,slkd->skgd", probs, value_view, preferred_element_type=jnp.float32)
    mixed = mixed + own_prob.astype(jnp.float32)[..., None] * new_value.reshape(
        seq_count, KVH, 1, HEAD
    ).astype(jnp.float32)
    return mixed.reshape(seq_count, QH * HEAD).astype(jnp.bfloat16)


def per_device(
    skip_stream,
    attention_probes,
    stored_attention_lookups,
    stored_attention_contents,
    incoming_lookup_entries,
    incoming_content_entries,
    filled_slot_spans,
    layernorm_gain,
    routed_specialist_indices,
    routing_probabilities,
    admission_limits,
    swap_indicator,
    gating_projection_matrix,
    widening_projection_matrix,
    output_projection_matrix,
):
    experts = lax.axis_size("expert")
    groups = lax.axis_size("dp")
    half_axis = experts // 2
    far_bit = experts.bit_length() - 2
    my_index = lax.axis_index("expert")
    my_device = my_index * groups + lax.axis_index("dp")
    own_weights = (
        gating_projection_matrix[0],
        widening_projection_matrix[0],
        output_projection_matrix[0],
    )
    partner = swapped(own_weights, "expert", far_bit)
    take_other = swap_indicator[my_index] == 1
    retained_specialist = jnp.where(take_other, (my_index + half_axis) % experts, my_index)

    seq_rows = skip_stream.shape[0]
    width = skip_stream.shape[1]
    slot_cap = 2
    side_cols = 128
    expert_range = lax.broadcasted_iota(jnp.int32, (experts,), 0)

    attn = attention(
        attention_probes,
        stored_attention_lookups,
        stored_attention_contents,
        incoming_lookup_entries,
        incoming_content_entries,
        filled_slot_spans,
    )
    stream = skip_stream.astype(jnp.float32) + attn.astype(jnp.float32)
    normed = (
        stream
        * lax.rsqrt(jnp.mean(stream * stream, axis=-1, keepdims=True) + 1e-06)
        * layernorm_gain
    ).astype(jnp.bfloat16)

    route_hot = (routed_specialist_indices[:, :, None] == expert_range[None, None, :]).astype(
        jnp.int32
    )
    row_hot = jnp.sum(route_hot, axis=1)
    earlier = jnp.cumsum(row_hot, axis=0) - row_hot
    local_rank = jnp.sum(route_hot * earlier[:, None, :], axis=-1)
    slot_code = routed_specialist_indices * slot_cap + local_rank
    targets = lax.broadcasted_iota(jnp.int32, (experts * slot_cap,), 0)
    slot_hits = jnp.any(slot_code[:, :, None] == targets[None, None, :], axis=1)
    occupied = jnp.any(slot_hits, axis=0)
    row_range = lax.broadcasted_iota(jnp.int32, (seq_rows, 1), 0)
    source_row = jnp.sum(jnp.where(slot_hits, row_range, 0), axis=0) + jnp.where(
        occupied, 0, seq_rows
    )
    padded_rows = jnp.concatenate([normed, jnp.zeros((1, width), jnp.bfloat16)], axis=0)
    outgoing = padded_rows[source_row].reshape(experts, slot_cap, width)
    partner_hist = jnp.roll(jnp.sum(row_hot, axis=0), -half_axis)
    col = lax.broadcasted_iota(jnp.int32, (experts, slot_cap, side_cols), 2)
    slot_of = lax.broadcasted_iota(jnp.int32, (experts, slot_cap, side_cols), 1)
    side = jnp.where(
        col == 0,
        occupied.reshape(experts, slot_cap, 1).astype(jnp.float32),
        jnp.where(
            (col == 1) & (slot_of == 0), partner_hist[:, None, None].astype(jnp.float32), 0.0
        ),
    ).astype(jnp.bfloat16)
    payload = jnp.concatenate([outgoing, side], axis=-1)
    own_down = own_weights[2]
    down_blocks = [own_down] + [
        lax.ppermute(own_down, "dp", [(j, (j + k) % groups) for j in range(groups)])
        for k in range(1, groups)
    ]
    arrived = lax.all_to_all(payload, "expert", split_axis=0, concat_axis=0, tiled=True)
    arrived, down_blocks = lax.optimization_barrier((arrived, down_blocks))
    down_shifted = jnp.stack(down_blocks, axis=0)
    column = lax.all_gather(arrived[None], "dp", axis=0, tiled=True)
    marks = column[:, :, :, width].astype(jnp.float32)
    partner_total = jnp.sum(column[:, :, :, width + 1].astype(jnp.float32))
    occupied_flat = jnp.transpose(marks, (1, 0, 2)).reshape(-1)
    before_count = jnp.cumsum(occupied_flat) - occupied_flat
    kept_flat = occupied_flat * (
        before_count < admission_limits[my_index].astype(jnp.float32)
    ).astype(jnp.float32)
    kept_mask = jnp.transpose(kept_flat.reshape(experts, groups, slot_cap), (1, 0, 2))
    own_total = jnp.sum(occupied_flat)
    held_tally = jnp.where(take_other, partner_total, own_total)
    device_share = jnp.minimum(
        held_tally, admission_limits[retained_specialist].astype(jnp.float32)
    ) / (seq_rows * routed_specialist_indices.shape[1] * groups)

    side_pad = ((0, 0), (0, side_cols))
    gate_wide = jnp.pad(own_weights[0], side_pad)
    up_wide = jnp.pad(own_weights[1], side_pad)
    gate_val = jnp.einsum(
        "desf,hf->desh", column, gate_wide, preferred_element_type=jnp.float32
    )
    up_val = jnp.einsum("desf,hf->desh", column, up_wide, preferred_element_type=jnp.float32)
    hidden = (jax.nn.silu(gate_val) * up_val).astype(jnp.bfloat16)
    hidden_kept = hidden * kept_mask[..., None].astype(jnp.bfloat16)
    unit_count = hidden_kept.shape[-1]
    hidden_col = lax.all_to_all(hidden_kept, "dp", split_axis=0, concat_axis=3, tiled=True)[0]
    summed = jnp.einsum(
        "esn,knf->eskf", hidden_col, down_shifted, preferred_element_type=jnp.float32
    )
    block_of = (lax.axis_index("dp") - lax.broadcasted_iota(jnp.int32, (groups,), 0)) % groups
    summed = jnp.take(summed.astype(jnp.bfloat16), block_of, axis=2)
    results = summed.reshape(experts, slot_cap, width)
    returned = lax.all_to_all(results, "expert", split_axis=0, concat_axis=0, tiled=True)
    returned_flat = returned.reshape(experts * slot_cap, width)
    picked = returned_flat[slot_code]
    expert_mix = jnp.sum(routing_probabilities[:, :, None] * picked.astype(jnp.float32), axis=1)
    layer_out = (stream + expert_mix).astype(jnp.bfloat16)
    gate_held = jnp.where(take_other, partner[0], own_weights[0])
    up_held = jnp.where(take_other, partner[1], own_weights[1])
    down_held = jnp.where(take_other, partner[2], own_weights[2])
    return (layer_out, device_share.reshape(1), gate_held[None], up_held[None], down_held[None])


def solution(mesh):
    in_specs = (
        P(("expert", "dp"), None),
        P(("expert", "dp"), None),
        P(("expert", "dp"), None, None),
        P(("expert", "dp"), None, None),
        P(("expert", "dp"), None),
        P(("expert", "dp"), None),
        P(("expert", "dp")),
        P(),
        P(("expert", "dp"), None),
        P(("expert", "dp"), None),
        P(),
        P(),
        P("expert", "dp", None),
        P("expert", "dp", None),
        P("expert", None, "dp"),
    )
    out_specs = (
        P(("expert", "dp"), None),
        P("expert"),
        P("expert", "dp", None),
        P("expert", "dp", None),
        P("expert", None, "dp"),
    )
    return jax.shard_map(
        per_device, mesh=mesh, in_specs=in_specs, out_specs=out_specs, check_vma=False
    )
```

```python
import jax
import jax.numpy as jnp
from jax import lax
from jax.sharding import PartitionSpec as P

QH = 32
KVH = 4
HEAD = 128


def swapped(value, axis, stride):
    mask = 2**stride
    pairs = [(source, source ^ mask) for source in range(lax.axis_size(axis))]
    return lax.ppermute(value, axis, pairs)


def attention(query_rows, key_rows, value_rows, new_key, new_value, valid_len):
    seq_count = query_rows.shape[0]
    cache_len = key_rows.shape[1]
    group = QH // KVH
    scale = HEAD ** (-0.5)
    query_view = query_rows.reshape(seq_count, KVH, group, HEAD)
    key_view = key_rows.reshape(seq_count, cache_len, KVH, HEAD)
    value_view = value_rows.reshape(seq_count, cache_len, KVH, HEAD)
    scores = (
        jnp.einsum("skgd,slkd->skgl", query_view, key_view, preferred_element_type=jnp.float32)
        * scale
    )
    valid = lax.broadcasted_iota(jnp.int32, (seq_count, cache_len), 1) < valid_len[:, None]
    scores = jnp.where(valid[:, None, None, :], scores, -1e30)
    own_score = (
        jnp.einsum(
            "skgd,skd->skg",
            query_view,
            new_key.reshape(seq_count, KVH, HEAD),
            preferred_element_type=jnp.float32,
        )
        * scale
    )
    highest = jnp.maximum(jnp.max(scores, axis=-1), own_score)
    weights = jnp.exp(scores - highest[..., None])
    own_weight = jnp.exp(own_score - highest)
    denom = jnp.sum(weights, axis=-1) + own_weight
    probs = (weights / denom[..., None]).astype(jnp.bfloat16)
    own_prob = (own_weight / denom).astype(jnp.bfloat16)
    mixed = jnp.einsum("skgl,slkd->skgd", probs, value_view, preferred_element_type=jnp.float32)
    mixed = mixed + own_prob.astype(jnp.float32)[..., None] * new_value.reshape(
        seq_count, KVH, 1, HEAD
    ).astype(jnp.float32)
    return mixed.reshape(seq_count, QH * HEAD).astype(jnp.bfloat16)


def per_device(
    skip_stream,
    attention_probes,
    stored_attention_lookups,
    stored_attention_contents,
    incoming_lookup_entries,
    incoming_content_entries,
    filled_slot_spans,
    layernorm_gain,
    routed_specialist_indices,
    routing_probabilities,
    admission_limits,
    swap_indicator,
    gating_projection_matrix,
    widening_projection_matrix,
    output_projection_matrix,
):
    experts = lax.axis_size("expert")
    groups = lax.axis_size("dp")
    half_axis = experts // 2
    far_bit = experts.bit_length() - 2
    my_index = lax.axis_index("expert")
    my_device = my_index * groups + lax.axis_index("dp")
    own_weights = (
        gating_projection_matrix[0],
        widening_projection_matrix[0],
        output_projection_matrix[0],
    )
    partner = swapped(own_weights, "expert", far_bit)
    take_other = swap_indicator[my_index] == 1
    retained_specialist = jnp.where(take_other, (my_index + half_axis) % experts, my_index)

    seq_rows = skip_stream.shape[0]
    width = skip_stream.shape[1]
    slot_cap = 2
    side_cols = 128
    expert_range = lax.broadcasted_iota(jnp.int32, (experts,), 0)

    attn = attention(
        attention_probes,
        stored_attention_lookups,
        stored_attention_contents,
        incoming_lookup_entries,
        incoming_content_entries,
        filled_slot_spans,
    )
    stream = skip_stream.astype(jnp.float32) + attn.astype(jnp.float32)
    normed = (
        stream
        * lax.rsqrt(jnp.mean(stream * stream, axis=-1, keepdims=True) + 1e-06)
        * layernorm_gain
    ).astype(jnp.bfloat16)

    route_hot = (routed_specialist_indices[:, :, None] == expert_range[None, None, :]).astype(
        jnp.int32
    )
    row_hot = jnp.sum(route_hot, axis=1)
    earlier = jnp.cumsum(row_hot, axis=0) - row_hot
    local_rank = jnp.sum(route_hot * earlier[:, None, :], axis=-1)
    slot_code = routed_specialist_indices * slot_cap + local_rank
    targets = lax.broadcasted_iota(jnp.int32, (experts * slot_cap,), 0)
    slot_hits = jnp.any(slot_code[:, :, None] == targets[None, None, :], axis=1)
    occupied = jnp.any(slot_hits, axis=0)
    row_range = lax.broadcasted_iota(jnp.int32, (seq_rows, 1), 0)
    source_row = jnp.sum(jnp.where(slot_hits, row_range, 0), axis=0) + jnp.where(
        occupied, 0, seq_rows
    )
    padded_rows = jnp.concatenate([normed, jnp.zeros((1, width), jnp.bfloat16)], axis=0)
    outgoing = padded_rows[source_row].reshape(experts, slot_cap, width)
    partner_hist = jnp.roll(jnp.sum(row_hot, axis=0), -half_axis)
    col = lax.broadcasted_iota(jnp.int32, (experts, slot_cap, side_cols), 2)
    slot_of = lax.broadcasted_iota(jnp.int32, (experts, slot_cap, side_cols), 1)
    side = jnp.where(
        col == 0,
        occupied.reshape(experts, slot_cap, 1).astype(jnp.float32),
        jnp.where(
            (col == 1) & (slot_of == 0), partner_hist[:, None, None].astype(jnp.float32), 0.0
        ),
    ).astype(jnp.bfloat16)
    payload = jnp.concatenate([outgoing, side], axis=-1)
    arrived = lax.all_to_all(payload, "expert", split_axis=0, concat_axis=0, tiled=True)
    arrived, partner = lax.optimization_barrier((arrived, partner))
    column = lax.all_gather(arrived[None], "dp", axis=0, tiled=True)
    marks = column[:, :, :, width].astype(jnp.float32)
    partner_total = jnp.sum(column[:, :, :, width + 1].astype(jnp.float32))
    occupied_flat = jnp.transpose(marks, (1, 0, 2)).reshape(-1)
    before_count = jnp.cumsum(occupied_flat) - occupied_flat
    kept_flat = occupied_flat * (
        before_count < admission_limits[my_index].astype(jnp.float32)
    ).astype(jnp.float32)
    kept_mask = jnp.transpose(kept_flat.reshape(experts, groups, slot_cap), (1, 0, 2))
    own_total = jnp.sum(occupied_flat)
    held_tally = jnp.where(take_other, partner_total, own_total)
    device_share = jnp.minimum(
        held_tally, admission_limits[retained_specialist].astype(jnp.float32)
    ) / (seq_rows * routed_specialist_indices.shape[1] * groups)

    side_pad = ((0, 0), (0, side_cols))
    gate_wide = jnp.pad(own_weights[0], side_pad)
    up_wide = jnp.pad(own_weights[1], side_pad)
    gate_val = jnp.einsum(
        "desf,hf->desh", column, gate_wide, preferred_element_type=jnp.float32
    )
    up_val = jnp.einsum("desf,hf->desh", column, up_wide, preferred_element_type=jnp.float32)
    hidden = (jax.nn.silu(gate_val) * up_val).astype(jnp.bfloat16)
    hidden_kept = hidden * kept_mask[..., None].astype(jnp.bfloat16)
    unit_count = hidden_kept.shape[-1]
    hidden_all = lax.all_gather(
        hidden_kept.reshape(1, groups * experts * slot_cap, unit_count), "dp", axis=0, tiled=True
    )
    feature_cols = own_weights[2].shape[1]
    down_split = own_weights[2].reshape(groups, unit_count, feature_cols)
    summed = jnp.einsum(
        "gsn,gnf->sf", hidden_all, down_split, preferred_element_type=jnp.float32
    )
    results = summed.astype(jnp.bfloat16).reshape(groups, experts, slot_cap, feature_cols)
    returned = lax.all_to_all(
        lax.all_to_all(results, "expert", split_axis=1, concat_axis=1, tiled=True),
        "dp",
        split_axis=0,
        concat_axis=3,
        tiled=True,
    )
    returned_flat = returned.reshape(experts * slot_cap, width)
    picked = returned_flat[slot_code]
    expert_mix = jnp.sum(routing_probabilities[:, :, None] * picked.astype(jnp.float32), axis=1)
    layer_out = (stream + expert_mix).astype(jnp.bfloat16)
    gate_held = jnp.where(take_other, partner[0], own_weights[0])
    up_held = jnp.where(take_other, partner[1], own_weights[1])
    down_held = jnp.where(take_other, partner[2], own_weights[2])
    return (layer_out, device_share.reshape(1), gate_held[None], up_held[None], down_held[None])


def solution(mesh):
    in_specs = (
        P(("expert", "dp"), None),
        P(("expert", "dp"), None),
        P(("expert", "dp"), None, None),
        P(("expert", "dp"), None, None),
        P(("expert", "dp"), None),
        P(("expert", "dp"), None),
        P(("expert", "dp")),
        P(),
        P(("expert", "dp"), None),
        P(("expert", "dp"), None),
        P(),
        P(),
        P("expert", "dp", None),
        P("expert", "dp", None),
        P("expert", None, "dp"),
    )
    out_specs = (
        P(("expert", "dp"), None),
        P("expert"),
        P("expert", "dp", None),
        P("expert", "dp", None),
        P("expert", None, "dp"),
    )
    return jax.shard_map(
        per_device, mesh=mesh, in_specs=in_specs, out_specs=out_specs, check_vma=False
    )
```

```python
import jax
import jax.numpy as jnp
from jax import lax
from jax.sharding import PartitionSpec as P

QH = 32
KVH = 4
HEAD = 128


def swapped(value, axis, stride):
    mask = 2**stride
    pairs = [(source, source ^ mask) for source in range(lax.axis_size(axis))]
    return lax.ppermute(value, axis, pairs)


def attention(query_rows, key_rows, value_rows, new_key, new_value, valid_len):
    seq_count = query_rows.shape[0]
    cache_len = key_rows.shape[1]
    group = QH // KVH
    scale = HEAD ** (-0.5)
    query_view = query_rows.reshape(seq_count, KVH, group, HEAD)
    key_view = key_rows.reshape(seq_count, cache_len, KVH, HEAD)
    value_view = value_rows.reshape(seq_count, cache_len, KVH, HEAD)
    scores = (
        jnp.einsum("skgd,slkd->skgl", query_view, key_view, preferred_element_type=jnp.float32)
        * scale
    )
    valid = lax.broadcasted_iota(jnp.int32, (seq_count, cache_len), 1) < valid_len[:, None]
    scores = jnp.where(valid[:, None, None, :], scores, -1e30)
    own_score = (
        jnp.einsum(
            "skgd,skd->skg",
            query_view,
            new_key.reshape(seq_count, KVH, HEAD),
            preferred_element_type=jnp.float32,
        )
        * scale
    )
    highest = jnp.maximum(jnp.max(scores, axis=-1), own_score)
    weights = jnp.exp(scores - highest[..., None])
    own_weight = jnp.exp(own_score - highest)
    denom = jnp.sum(weights, axis=-1) + own_weight
    probs = (weights / denom[..., None]).astype(jnp.bfloat16)
    own_prob = (own_weight / denom).astype(jnp.bfloat16)
    mixed = jnp.einsum("skgl,slkd->skgd", probs, value_view, preferred_element_type=jnp.float32)
    mixed = mixed + own_prob.astype(jnp.float32)[..., None] * new_value.reshape(
        seq_count, KVH, 1, HEAD
    ).astype(jnp.float32)
    return mixed.reshape(seq_count, QH * HEAD).astype(jnp.bfloat16)


def per_device(
    skip_stream,
    attention_probes,
    stored_attention_lookups,
    stored_attention_contents,
    incoming_lookup_entries,
    incoming_content_entries,
    filled_slot_spans,
    layernorm_gain,
    routed_specialist_indices,
    routing_probabilities,
    admission_limits,
    swap_indicator,
    gating_projection_matrix,
    widening_projection_matrix,
    output_projection_matrix,
):
    experts = lax.axis_size("expert")
    groups = lax.axis_size("dp")
    half_axis = experts // 2
    far_bit = experts.bit_length() - 2
    my_index = lax.axis_index("expert")
    my_device = my_index * groups + lax.axis_index("dp")
    own_weights = (
        gating_projection_matrix[0],
        widening_projection_matrix[0],
        output_projection_matrix[0],
    )
    partner = swapped(own_weights, "expert", far_bit)
    take_other = swap_indicator[my_index] == 1
    retained_specialist = jnp.where(take_other, (my_index + half_axis) % experts, my_index)

    seq_rows = skip_stream.shape[0]
    width = skip_stream.shape[1]
    slot_cap = 2
    side_cols = 128
    expert_range = lax.broadcasted_iota(jnp.int32, (experts,), 0)

    attn = attention(
        attention_probes,
        stored_attention_lookups,
        stored_attention_contents,
        incoming_lookup_entries,
        incoming_content_entries,
        filled_slot_spans,
    )
    stream = skip_stream.astype(jnp.float32) + attn.astype(jnp.float32)
    normed = (
        stream
        * lax.rsqrt(jnp.mean(stream * stream, axis=-1, keepdims=True) + 1e-06)
        * layernorm_gain
    ).astype(jnp.bfloat16)

    route_hot = (routed_specialist_indices[:, :, None] == expert_range[None, None, :]).astype(
        jnp.int32
    )
    row_hot = jnp.sum(route_hot, axis=1)
    earlier = jnp.cumsum(row_hot, axis=0) - row_hot
    local_rank = jnp.sum(route_hot * earlier[:, None, :], axis=-1)
    slot_code = routed_specialist_indices * slot_cap + local_rank
    targets = lax.broadcasted_iota(jnp.int32, (experts * slot_cap,), 0)
    slot_hits = jnp.any(slot_code[:, :, None] == targets[None, None, :], axis=1)
    occupied = jnp.any(slot_hits, axis=0)
    row_range = lax.broadcasted_iota(jnp.int32, (seq_rows, 1), 0)
    source_row = jnp.sum(jnp.where(slot_hits, row_range, 0), axis=0) + jnp.where(
        occupied, 0, seq_rows
    )
    padded_rows = jnp.concatenate([normed, jnp.zeros((1, width), jnp.bfloat16)], axis=0)
    outgoing = padded_rows[source_row].reshape(experts, slot_cap, width)
    partner_hist = jnp.roll(jnp.sum(row_hot, axis=0), -half_axis)
    col = lax.broadcasted_iota(jnp.int32, (experts, slot_cap, side_cols), 2)
    slot_of = lax.broadcasted_iota(jnp.int32, (experts, slot_cap, side_cols), 1)
    side = jnp.where(
        col == 0,
        occupied.reshape(experts, slot_cap, 1).astype(jnp.float32),
        jnp.where(
            (col == 1) & (slot_of == 0), partner_hist[:, None, None].astype(jnp.float32), 0.0
        ),
    ).astype(jnp.bfloat16)
    payload = jnp.concatenate([outgoing, side], axis=-1)
    arrived = lax.all_to_all(payload, "expert", split_axis=0, concat_axis=0, tiled=True)
    column = lax.all_gather(arrived[None], "dp", axis=0, tiled=True)
    marks = column[:, :, :, width].astype(jnp.float32)
    partner_total = jnp.sum(column[:, :, :, width + 1].astype(jnp.float32))
    occupied_flat = jnp.transpose(marks, (1, 0, 2)).reshape(-1)
    before_count = jnp.cumsum(occupied_flat) - occupied_flat
    kept_flat = occupied_flat * (
        before_count < admission_limits[my_index].astype(jnp.float32)
    ).astype(jnp.float32)
    kept_mask = jnp.transpose(kept_flat.reshape(experts, groups, slot_cap), (1, 0, 2))
    own_total = jnp.sum(occupied_flat)
    held_tally = jnp.where(take_other, partner_total, own_total)
    device_share = jnp.minimum(
        held_tally, admission_limits[retained_specialist].astype(jnp.float32)
    ) / (seq_rows * routed_specialist_indices.shape[1] * groups)

    side_pad = ((0, 0), (0, side_cols))
    gate_wide = jnp.pad(own_weights[0], side_pad)
    up_wide = jnp.pad(own_weights[1], side_pad)
    gate_val = jnp.einsum(
        "desf,hf->desh", column, gate_wide, preferred_element_type=jnp.float32
    )
    up_val = jnp.einsum("desf,hf->desh", column, up_wide, preferred_element_type=jnp.float32)
    hidden = (jax.nn.silu(gate_val) * up_val).astype(jnp.bfloat16)
    hidden_kept = hidden * kept_mask[..., None].astype(jnp.bfloat16)
    unit_count = hidden_kept.shape[-1]
    hidden_block = hidden_kept.reshape(1, groups * experts * slot_cap, unit_count)
    hidden_all = lax.all_to_all(
        jnp.broadcast_to(hidden_block, (groups,) + hidden_block.shape[1:]),
        "dp",
        split_axis=0,
        concat_axis=0,
        tiled=True,
    )
    feature_cols = own_weights[2].shape[1]
    down_split = own_weights[2].reshape(groups, unit_count, feature_cols)
    summed = jnp.einsum(
        "gsn,gnf->sf", hidden_all, down_split, preferred_element_type=jnp.float32
    )
    results = summed.astype(jnp.bfloat16).reshape(groups, experts, slot_cap, feature_cols)
    returned = lax.all_to_all(
        lax.all_to_all(results, "expert", split_axis=1, concat_axis=1, tiled=True),
        "dp",
        split_axis=0,
        concat_axis=3,
        tiled=True,
    )
    returned_flat = returned.reshape(experts * slot_cap, width)
    picked = returned_flat[slot_code]
    expert_mix = jnp.sum(routing_probabilities[:, :, None] * picked.astype(jnp.float32), axis=1)
    layer_out = (stream + expert_mix).astype(jnp.bfloat16)
    gate_held = jnp.where(take_other, partner[0], own_weights[0])
    up_held = jnp.where(take_other, partner[1], own_weights[1])
    down_held = jnp.where(take_other, partner[2], own_weights[2])
    return (layer_out, device_share.reshape(1), gate_held[None], up_held[None], down_held[None])


def solution(mesh):
    in_specs = (
        P(("expert", "dp"), None),
        P(("expert", "dp"), None),
        P(("expert", "dp"), None, None),
        P(("expert", "dp"), None, None),
        P(("expert", "dp"), None),
        P(("expert", "dp"), None),
        P(("expert", "dp")),
        P(),
        P(("expert", "dp"), None),
        P(("expert", "dp"), None),
        P(),
        P(),
        P("expert", "dp", None),
        P("expert", "dp", None),
        P("expert", None, "dp"),
    )
    out_specs = (
        P(("expert", "dp"), None),
        P("expert"),
        P("expert", "dp", None),
        P("expert", "dp", None),
        P("expert", None, "dp"),
    )
    return jax.shard_map(
        per_device, mesh=mesh, in_specs=in_specs, out_specs=out_specs, check_vma=False
    )
```

```python
import jax
import jax.numpy as jnp
from jax import lax
from jax.sharding import PartitionSpec as P

QH = 32
KVH = 4
HEAD = 128


def swapped(value, axis, stride):
    mask = 2**stride
    pairs = [(source, source ^ mask) for source in range(lax.axis_size(axis))]
    return lax.ppermute(value, axis, pairs)


def attention(query_rows, key_rows, value_rows, new_key, new_value, valid_len):
    seq_count = query_rows.shape[0]
    cache_len = key_rows.shape[1]
    group = QH // KVH
    scale = HEAD ** (-0.5)
    query_view = query_rows.reshape(seq_count, KVH, group, HEAD)
    key_view = key_rows.reshape(seq_count, cache_len, KVH, HEAD)
    value_view = value_rows.reshape(seq_count, cache_len, KVH, HEAD)
    scores = (
        jnp.einsum("skgd,slkd->skgl", query_view, key_view, preferred_element_type=jnp.float32)
        * scale
    )
    valid = lax.broadcasted_iota(jnp.int32, (seq_count, cache_len), 1) < valid_len[:, None]
    scores = jnp.where(valid[:, None, None, :], scores, -1e30)
    own_score = (
        jnp.einsum(
            "skgd,skd->skg",
            query_view,
            new_key.reshape(seq_count, KVH, HEAD),
            preferred_element_type=jnp.float32,
        )
        * scale
    )
    highest = jnp.maximum(jnp.max(scores, axis=-1), own_score)
    weights = jnp.exp(scores - highest[..., None])
    own_weight = jnp.exp(own_score - highest)
    denom = jnp.sum(weights, axis=-1) + own_weight
    probs = (weights / denom[..., None]).astype(jnp.bfloat16)
    own_prob = (own_weight / denom).astype(jnp.bfloat16)
    mixed = jnp.einsum("skgl,slkd->skgd", probs, value_view, preferred_element_type=jnp.float32)
    mixed = mixed + own_prob.astype(jnp.float32)[..., None] * new_value.reshape(
        seq_count, KVH, 1, HEAD
    ).astype(jnp.float32)
    return mixed.reshape(seq_count, QH * HEAD).astype(jnp.bfloat16)


def per_device(
    skip_stream,
    attention_probes,
    stored_attention_lookups,
    stored_attention_contents,
    incoming_lookup_entries,
    incoming_content_entries,
    filled_slot_spans,
    layernorm_gain,
    routed_specialist_indices,
    routing_probabilities,
    admission_limits,
    swap_indicator,
    gating_projection_matrix,
    widening_projection_matrix,
    output_projection_matrix,
):
    experts = lax.axis_size("expert")
    groups = lax.axis_size("dp")
    half_axis = experts // 2
    far_bit = experts.bit_length() - 2
    my_index = lax.axis_index("expert")
    my_device = my_index * groups + lax.axis_index("dp")
    own_weights = (
        gating_projection_matrix[0],
        widening_projection_matrix[0],
        output_projection_matrix[0],
    )
    partner = swapped(own_weights, "expert", far_bit)
    take_other = swap_indicator[my_index] == 1
    retained_specialist = jnp.where(take_other, (my_index + half_axis) % experts, my_index)

    seq_rows = skip_stream.shape[0]
    width = skip_stream.shape[1]
    slot_cap = 2
    side_cols = 128
    expert_range = lax.broadcasted_iota(jnp.int32, (experts,), 0)

    attn = attention(
        attention_probes,
        stored_attention_lookups,
        stored_attention_contents,
        incoming_lookup_entries,
        incoming_content_entries,
        filled_slot_spans,
    )
    stream = skip_stream.astype(jnp.float32) + attn.astype(jnp.float32)
    normed = (
        stream
        * lax.rsqrt(jnp.mean(stream * stream, axis=-1, keepdims=True) + 1e-06)
        * layernorm_gain
    ).astype(jnp.bfloat16)

    route_hot = (routed_specialist_indices[:, :, None] == expert_range[None, None, :]).astype(
        jnp.int32
    )
    row_hot = jnp.sum(route_hot, axis=1)
    earlier = jnp.cumsum(row_hot, axis=0) - row_hot
    local_rank = jnp.sum(route_hot * earlier[:, None, :], axis=-1)
    slot_code = routed_specialist_indices * slot_cap + local_rank
    targets = lax.broadcasted_iota(jnp.int32, (experts * slot_cap,), 0)
    slot_hits = jnp.any(slot_code[:, :, None] == targets[None, None, :], axis=1)
    occupied = jnp.any(slot_hits, axis=0)
    row_range = lax.broadcasted_iota(jnp.int32, (seq_rows, 1), 0)
    source_row = jnp.sum(jnp.where(slot_hits, row_range, 0), axis=0) + jnp.where(
        occupied, 0, seq_rows
    )
    padded_rows = jnp.concatenate([normed, jnp.zeros((1, width), jnp.bfloat16)], axis=0)
    outgoing = padded_rows[source_row].reshape(experts, slot_cap, width)
    partner_hist = jnp.roll(jnp.sum(row_hot, axis=0), -half_axis)
    col = lax.broadcasted_iota(jnp.int32, (experts, slot_cap, side_cols), 2)
    slot_of = lax.broadcasted_iota(jnp.int32, (experts, slot_cap, side_cols), 1)
    side = jnp.where(
        col == 0,
        occupied.reshape(experts, slot_cap, 1).astype(jnp.float32),
        jnp.where(
            (col == 1) & (slot_of == 0), partner_hist[:, None, None].astype(jnp.float32), 0.0
        ),
    ).astype(jnp.bfloat16)
    payload = jnp.concatenate([outgoing, side], axis=-1)
    arrived = lax.all_to_all(payload, "expert", split_axis=0, concat_axis=0, tiled=True)
    column = lax.all_to_all(
        jnp.broadcast_to(arrived[None], (groups,) + arrived.shape),
        "dp",
        split_axis=0,
        concat_axis=0,
        tiled=True,
    )
    marks = column[:, :, :, width].astype(jnp.float32)
    partner_total = jnp.sum(column[:, :, :, width + 1].astype(jnp.float32))
    occupied_flat = jnp.transpose(marks, (1, 0, 2)).reshape(-1)
    before_count = jnp.cumsum(occupied_flat) - occupied_flat
    kept_flat = occupied_flat * (
        before_count < admission_limits[my_index].astype(jnp.float32)
    ).astype(jnp.float32)
    kept_mask = jnp.transpose(kept_flat.reshape(experts, groups, slot_cap), (1, 0, 2))
    own_total = jnp.sum(occupied_flat)
    held_tally = jnp.where(take_other, partner_total, own_total)
    device_share = jnp.minimum(
        held_tally, admission_limits[retained_specialist].astype(jnp.float32)
    ) / (seq_rows * routed_specialist_indices.shape[1] * groups)

    side_pad = ((0, 0), (0, side_cols))
    gate_wide = jnp.pad(own_weights[0], side_pad)
    up_wide = jnp.pad(own_weights[1], side_pad)
    gate_val = jnp.einsum(
        "desf,hf->desh", column, gate_wide, preferred_element_type=jnp.float32
    )
    up_val = jnp.einsum("desf,hf->desh", column, up_wide, preferred_element_type=jnp.float32)
    hidden = (jax.nn.silu(gate_val) * up_val).astype(jnp.bfloat16)
    hidden_kept = hidden * kept_mask[..., None].astype(jnp.bfloat16)
    unit_count = hidden_kept.shape[-1]
    hidden_block = hidden_kept.reshape(1, groups * experts * slot_cap, unit_count)
    hidden_all = lax.all_to_all(
        jnp.broadcast_to(hidden_block, (groups,) + hidden_block.shape[1:]),
        "dp",
        split_axis=0,
        concat_axis=0,
        tiled=True,
    )
    feature_cols = own_weights[2].shape[1]
    down_split = own_weights[2].reshape(groups, unit_count, feature_cols)
    summed = jnp.einsum(
        "gsn,gnf->sf", hidden_all, down_split, preferred_element_type=jnp.float32
    )
    results = summed.astype(jnp.bfloat16).reshape(groups, experts, slot_cap, feature_cols)
    returned = lax.all_to_all(
        lax.all_to_all(results, "expert", split_axis=1, concat_axis=1, tiled=True),
        "dp",
        split_axis=0,
        concat_axis=3,
        tiled=True,
    )
    returned_flat = returned.reshape(experts * slot_cap, width)
    picked = returned_flat[slot_code]
    expert_mix = jnp.sum(routing_probabilities[:, :, None] * picked.astype(jnp.float32), axis=1)
    layer_out = (stream + expert_mix).astype(jnp.bfloat16)
    gate_held = jnp.where(take_other, partner[0], own_weights[0])
    up_held = jnp.where(take_other, partner[1], own_weights[1])
    down_held = jnp.where(take_other, partner[2], own_weights[2])
    return (layer_out, device_share.reshape(1), gate_held[None], up_held[None], down_held[None])


def solution(mesh):
    in_specs = (
        P(("expert", "dp"), None),
        P(("expert", "dp"), None),
        P(("expert", "dp"), None, None),
        P(("expert", "dp"), None, None),
        P(("expert", "dp"), None),
        P(("expert", "dp"), None),
        P(("expert", "dp")),
        P(),
        P(("expert", "dp"), None),
        P(("expert", "dp"), None),
        P(),
        P(),
        P("expert", "dp", None),
        P("expert", "dp", None),
        P("expert", None, "dp"),
    )
    out_specs = (
        P(("expert", "dp"), None),
        P("expert"),
        P("expert", "dp", None),
        P("expert", "dp", None),
        P("expert", None, "dp"),
    )
    return jax.shard_map(
        per_device, mesh=mesh, in_specs=in_specs, out_specs=out_specs, check_vma=False
    )
```

```python
import jax
import jax.numpy as jnp
from jax import lax
from jax.sharding import PartitionSpec as P

QH = 32
KVH = 4
HEAD = 128


def swapped(value, axis, stride):
    mask = 2**stride
    pairs = [(source, source ^ mask) for source in range(lax.axis_size(axis))]
    return lax.ppermute(value, axis, pairs)


def attention(query_rows, key_rows, value_rows, new_key, new_value, valid_len):
    seq_count = query_rows.shape[0]
    cache_len = key_rows.shape[1]
    group = QH // KVH
    scale = HEAD ** (-0.5)
    query_view = query_rows.reshape(seq_count, KVH, group, HEAD)
    key_view = key_rows.reshape(seq_count, cache_len, KVH, HEAD)
    value_view = value_rows.reshape(seq_count, cache_len, KVH, HEAD)
    scores = (
        jnp.einsum("skgd,slkd->skgl", query_view, key_view, preferred_element_type=jnp.float32)
        * scale
    )
    valid = lax.broadcasted_iota(jnp.int32, (seq_count, cache_len), 1) < valid_len[:, None]
    scores = jnp.where(valid[:, None, None, :], scores, -1e30)
    own_score = (
        jnp.einsum(
            "skgd,skd->skg",
            query_view,
            new_key.reshape(seq_count, KVH, HEAD),
            preferred_element_type=jnp.float32,
        )
        * scale
    )
    highest = jnp.maximum(jnp.max(scores, axis=-1), own_score)
    weights = jnp.exp(scores - highest[..., None])
    own_weight = jnp.exp(own_score - highest)
    denom = jnp.sum(weights, axis=-1) + own_weight
    probs = (weights / denom[..., None]).astype(jnp.bfloat16)
    own_prob = (own_weight / denom).astype(jnp.bfloat16)
    mixed = jnp.einsum("skgl,slkd->skgd", probs, value_view, preferred_element_type=jnp.float32)
    mixed = mixed + own_prob.astype(jnp.float32)[..., None] * new_value.reshape(
        seq_count, KVH, 1, HEAD
    ).astype(jnp.float32)
    return mixed.reshape(seq_count, QH * HEAD).astype(jnp.bfloat16)


def per_device(
    skip_stream,
    attention_probes,
    stored_attention_lookups,
    stored_attention_contents,
    incoming_lookup_entries,
    incoming_content_entries,
    filled_slot_spans,
    layernorm_gain,
    routed_specialist_indices,
    routing_probabilities,
    admission_limits,
    swap_indicator,
    gating_projection_matrix,
    widening_projection_matrix,
    output_projection_matrix,
):
    experts = lax.axis_size("expert")
    groups = lax.axis_size("dp")
    half_axis = experts // 2
    far_bit = experts.bit_length() - 2
    my_index = lax.axis_index("expert")
    my_device = my_index * groups + lax.axis_index("dp")
    own_weights = (
        gating_projection_matrix[0],
        widening_projection_matrix[0],
        output_projection_matrix[0],
    )
    packed = jnp.concatenate([w.reshape(-1) for w in own_weights])
    arrived_weights = swapped(packed, "expert", far_bit)
    sizes = [w.size for w in own_weights]
    partner = (
        arrived_weights[: sizes[0]].reshape(own_weights[0].shape),
        arrived_weights[sizes[0] : sizes[0] + sizes[1]].reshape(own_weights[1].shape),
        arrived_weights[sizes[0] + sizes[1] :].reshape(own_weights[2].shape),
    )
    take_other = swap_indicator[my_index] == 1
    retained_specialist = jnp.where(take_other, (my_index + half_axis) % experts, my_index)

    seq_rows = skip_stream.shape[0]
    width = skip_stream.shape[1]
    slot_cap = 2
    side_cols = 128
    expert_range = lax.broadcasted_iota(jnp.int32, (experts,), 0)

    attn = attention(
        attention_probes,
        stored_attention_lookups,
        stored_attention_contents,
        incoming_lookup_entries,
        incoming_content_entries,
        filled_slot_spans,
    )
    stream = skip_stream.astype(jnp.float32) + attn.astype(jnp.float32)
    normed = (
        stream
        * lax.rsqrt(jnp.mean(stream * stream, axis=-1, keepdims=True) + 1e-06)
        * layernorm_gain
    ).astype(jnp.bfloat16)

    route_hot = (routed_specialist_indices[:, :, None] == expert_range[None, None, :]).astype(
        jnp.int32
    )
    row_hot = jnp.sum(route_hot, axis=1)
    earlier = jnp.cumsum(row_hot, axis=0) - row_hot
    local_rank = jnp.sum(route_hot * earlier[:, None, :], axis=-1)
    slot_code = routed_specialist_indices * slot_cap + local_rank
    targets = lax.broadcasted_iota(jnp.int32, (experts * slot_cap,), 0)
    slot_hits = jnp.any(slot_code[:, :, None] == targets[None, None, :], axis=1)
    occupied = jnp.any(slot_hits, axis=0)
    row_range = lax.broadcasted_iota(jnp.int32, (seq_rows, 1), 0)
    source_row = jnp.sum(jnp.where(slot_hits, row_range, 0), axis=0) + jnp.where(
        occupied, 0, seq_rows
    )
    padded_rows = jnp.concatenate([normed, jnp.zeros((1, width), jnp.bfloat16)], axis=0)
    outgoing = padded_rows[source_row].reshape(experts, slot_cap, width)
    partner_hist = jnp.roll(jnp.sum(row_hot, axis=0), -half_axis)
    col = lax.broadcasted_iota(jnp.int32, (experts, slot_cap, side_cols), 2)
    slot_of = lax.broadcasted_iota(jnp.int32, (experts, slot_cap, side_cols), 1)
    side = jnp.where(
        col == 0,
        occupied.reshape(experts, slot_cap, 1).astype(jnp.float32),
        jnp.where(
            (col == 1) & (slot_of == 0), partner_hist[:, None, None].astype(jnp.float32), 0.0
        ),
    ).astype(jnp.bfloat16)
    payload = jnp.concatenate([outgoing, side], axis=-1)
    arrived = lax.all_to_all(payload, "expert", split_axis=0, concat_axis=0, tiled=True)
    column = lax.all_to_all(
        jnp.broadcast_to(arrived[None], (groups,) + arrived.shape),
        "dp",
        split_axis=0,
        concat_axis=0,
        tiled=True,
    )
    marks = column[:, :, :, width].astype(jnp.float32)
    partner_total = jnp.sum(column[:, :, :, width + 1].astype(jnp.float32))
    occupied_flat = jnp.transpose(marks, (1, 0, 2)).reshape(-1)
    before_count = jnp.cumsum(occupied_flat) - occupied_flat
    kept_flat = occupied_flat * (
        before_count < admission_limits[my_index].astype(jnp.float32)
    ).astype(jnp.float32)
    kept_mask = jnp.transpose(kept_flat.reshape(experts, groups, slot_cap), (1, 0, 2))
    own_total = jnp.sum(occupied_flat)
    held_tally = jnp.where(take_other, partner_total, own_total)
    device_share = jnp.minimum(
        held_tally, admission_limits[retained_specialist].astype(jnp.float32)
    ) / (seq_rows * routed_specialist_indices.shape[1] * groups)

    side_pad = ((0, 0), (0, side_cols))
    gate_wide = jnp.pad(own_weights[0], side_pad)
    up_wide = jnp.pad(own_weights[1], side_pad)
    gate_val = jnp.einsum(
        "desf,hf->desh", column, gate_wide, preferred_element_type=jnp.float32
    )
    up_val = jnp.einsum("desf,hf->desh", column, up_wide, preferred_element_type=jnp.float32)
    hidden = (jax.nn.silu(gate_val) * up_val).astype(jnp.bfloat16)
    hidden_kept = hidden * kept_mask[..., None].astype(jnp.bfloat16)
    unit_count = hidden_kept.shape[-1]
    hidden_block = hidden_kept.reshape(1, groups * experts * slot_cap, unit_count)
    hidden_all = lax.all_to_all(
        jnp.broadcast_to(hidden_block, (groups,) + hidden_block.shape[1:]),
        "dp",
        split_axis=0,
        concat_axis=0,
        tiled=True,
    )
    feature_cols = own_weights[2].shape[1]
    down_split = own_weights[2].reshape(groups, unit_count, feature_cols)
    summed = jnp.einsum(
        "gsn,gnf->sf", hidden_all, down_split, preferred_element_type=jnp.float32
    )
    results = summed.astype(jnp.bfloat16).reshape(groups, experts, slot_cap, feature_cols)
    returned = lax.all_to_all(
        lax.all_to_all(results, "expert", split_axis=1, concat_axis=1, tiled=True),
        "dp",
        split_axis=0,
        concat_axis=3,
        tiled=True,
    )
    returned_flat = returned.reshape(experts * slot_cap, width)
    picked = returned_flat[slot_code]
    expert_mix = jnp.sum(routing_probabilities[:, :, None] * picked.astype(jnp.float32), axis=1)
    layer_out = (stream + expert_mix).astype(jnp.bfloat16)
    gate_held = jnp.where(take_other, partner[0], own_weights[0])
    up_held = jnp.where(take_other, partner[1], own_weights[1])
    down_held = jnp.where(take_other, partner[2], own_weights[2])
    return (layer_out, device_share.reshape(1), gate_held[None], up_held[None], down_held[None])


def solution(mesh):
    in_specs = (
        P(("expert", "dp"), None),
        P(("expert", "dp"), None),
        P(("expert", "dp"), None, None),
        P(("expert", "dp"), None, None),
        P(("expert", "dp"), None),
        P(("expert", "dp"), None),
        P(("expert", "dp")),
        P(),
        P(("expert", "dp"), None),
        P(("expert", "dp"), None),
        P(),
        P(),
        P("expert", "dp", None),
        P("expert", "dp", None),
        P("expert", None, "dp"),
    )
    out_specs = (
        P(("expert", "dp"), None),
        P("expert"),
        P("expert", "dp", None),
        P("expert", "dp", None),
        P("expert", None, "dp"),
    )
    return jax.shard_map(
        per_device, mesh=mesh, in_specs=in_specs, out_specs=out_specs, check_vma=False
    )
```

```python
import jax
import jax.numpy as jnp
from jax import lax
from jax.sharding import PartitionSpec as P

QH = 32
KVH = 4
HEAD = 128


def swapped(value, axis, stride):
    mask = 2**stride
    pairs = [(source, source ^ mask) for source in range(lax.axis_size(axis))]
    return lax.ppermute(value, axis, pairs)


def attention(query_rows, key_rows, value_rows, new_key, new_value, valid_len):
    seq_count = query_rows.shape[0]
    cache_len = key_rows.shape[1]
    group = QH // KVH
    scale = HEAD ** (-0.5)
    query_view = query_rows.reshape(seq_count, KVH, group, HEAD)
    key_view = key_rows.reshape(seq_count, cache_len, KVH, HEAD)
    value_view = value_rows.reshape(seq_count, cache_len, KVH, HEAD)
    scores = (
        jnp.einsum("skgd,slkd->skgl", query_view, key_view, preferred_element_type=jnp.float32)
        * scale
    )
    valid = lax.broadcasted_iota(jnp.int32, (seq_count, cache_len), 1) < valid_len[:, None]
    scores = jnp.where(valid[:, None, None, :], scores, -1e30)
    own_score = (
        jnp.einsum(
            "skgd,skd->skg",
            query_view,
            new_key.reshape(seq_count, KVH, HEAD),
            preferred_element_type=jnp.float32,
        )
        * scale
    )
    highest = jnp.maximum(jnp.max(scores, axis=-1), own_score)
    weights = jnp.exp(scores - highest[..., None])
    own_weight = jnp.exp(own_score - highest)
    denom = jnp.sum(weights, axis=-1) + own_weight
    probs = (weights / denom[..., None]).astype(jnp.bfloat16)
    own_prob = (own_weight / denom).astype(jnp.bfloat16)
    mixed = jnp.einsum("skgl,slkd->skgd", probs, value_view, preferred_element_type=jnp.float32)
    mixed = mixed + own_prob.astype(jnp.float32)[..., None] * new_value.reshape(
        seq_count, KVH, 1, HEAD
    ).astype(jnp.float32)
    return mixed.reshape(seq_count, QH * HEAD).astype(jnp.bfloat16)


def per_device(
    skip_stream,
    attention_probes,
    stored_attention_lookups,
    stored_attention_contents,
    incoming_lookup_entries,
    incoming_content_entries,
    filled_slot_spans,
    layernorm_gain,
    routed_specialist_indices,
    routing_probabilities,
    admission_limits,
    swap_indicator,
    gating_projection_matrix,
    widening_projection_matrix,
    output_projection_matrix,
):
    experts = lax.axis_size("expert")
    groups = lax.axis_size("dp")
    half_axis = experts // 2
    far_bit = experts.bit_length() - 2
    my_index = lax.axis_index("expert")
    my_device = my_index * groups + lax.axis_index("dp")
    own_weights = (
        gating_projection_matrix[0],
        widening_projection_matrix[0],
        output_projection_matrix[0],
    )
    def x_step(direction):
        pairs = []
        for source in range(experts * groups):
            e, d = divmod(source, groups)
            x = 2 * (e // half_axis) + d // (groups // 2)
            nx = (x + direction) % 4
            e2 = (nx // 2) * half_axis + e % half_axis
            d2 = (nx % 2) * (groups // 2) + d % (groups // 2)
            pairs.append((source, e2 * groups + d2))
        return pairs

    both = ("expert", "dp")
    gate_far = lax.ppermute(lax.ppermute(own_weights[0], both, x_step(1)), both, x_step(1))
    up_far = lax.ppermute(lax.ppermute(own_weights[1], both, x_step(-1)), both, x_step(-1))
    partner = (gate_far, up_far, swapped(own_weights[2], "expert", far_bit))
    take_other = swap_indicator[my_index] == 1
    retained_specialist = jnp.where(take_other, (my_index + half_axis) % experts, my_index)

    seq_rows = skip_stream.shape[0]
    width = skip_stream.shape[1]
    slot_cap = 2
    side_cols = 128
    expert_range = lax.broadcasted_iota(jnp.int32, (experts,), 0)

    attn = attention(
        attention_probes,
        stored_attention_lookups,
        stored_attention_contents,
        incoming_lookup_entries,
        incoming_content_entries,
        filled_slot_spans,
    )
    stream = skip_stream.astype(jnp.float32) + attn.astype(jnp.float32)
    normed = (
        stream
        * lax.rsqrt(jnp.mean(stream * stream, axis=-1, keepdims=True) + 1e-06)
        * layernorm_gain
    ).astype(jnp.bfloat16)

    route_hot = (routed_specialist_indices[:, :, None] == expert_range[None, None, :]).astype(
        jnp.int32
    )
    row_hot = jnp.sum(route_hot, axis=1)
    earlier = jnp.cumsum(row_hot, axis=0) - row_hot
    local_rank = jnp.sum(route_hot * earlier[:, None, :], axis=-1)
    slot_code = routed_specialist_indices * slot_cap + local_rank
    targets = lax.broadcasted_iota(jnp.int32, (experts * slot_cap,), 0)
    slot_hits = jnp.any(slot_code[:, :, None] == targets[None, None, :], axis=1)
    occupied = jnp.any(slot_hits, axis=0)
    row_range = lax.broadcasted_iota(jnp.int32, (seq_rows, 1), 0)
    source_row = jnp.sum(jnp.where(slot_hits, row_range, 0), axis=0) + jnp.where(
        occupied, 0, seq_rows
    )
    padded_rows = jnp.concatenate([normed, jnp.zeros((1, width), jnp.bfloat16)], axis=0)
    outgoing = padded_rows[source_row].reshape(experts, slot_cap, width)
    partner_hist = jnp.roll(jnp.sum(row_hot, axis=0), -half_axis)
    col = lax.broadcasted_iota(jnp.int32, (experts, slot_cap, side_cols), 2)
    slot_of = lax.broadcasted_iota(jnp.int32, (experts, slot_cap, side_cols), 1)
    side = jnp.where(
        col == 0,
        occupied.reshape(experts, slot_cap, 1).astype(jnp.float32),
        jnp.where(
            (col == 1) & (slot_of == 0), partner_hist[:, None, None].astype(jnp.float32), 0.0
        ),
    ).astype(jnp.bfloat16)
    payload = jnp.concatenate([outgoing, side], axis=-1)
    arrived = lax.all_to_all(payload, "expert", split_axis=0, concat_axis=0, tiled=True)
    column = lax.all_to_all(
        jnp.broadcast_to(arrived[None], (groups,) + arrived.shape),
        "dp",
        split_axis=0,
        concat_axis=0,
        tiled=True,
    )
    marks = column[:, :, :, width].astype(jnp.float32)
    partner_total = jnp.sum(column[:, :, :, width + 1].astype(jnp.float32))
    occupied_flat = jnp.transpose(marks, (1, 0, 2)).reshape(-1)
    before_count = jnp.cumsum(occupied_flat) - occupied_flat
    kept_flat = occupied_flat * (
        before_count < admission_limits[my_index].astype(jnp.float32)
    ).astype(jnp.float32)
    kept_mask = jnp.transpose(kept_flat.reshape(experts, groups, slot_cap), (1, 0, 2))
    own_total = jnp.sum(occupied_flat)
    held_tally = jnp.where(take_other, partner_total, own_total)
    device_share = jnp.minimum(
        held_tally, admission_limits[retained_specialist].astype(jnp.float32)
    ) / (seq_rows * routed_specialist_indices.shape[1] * groups)

    side_pad = ((0, 0), (0, side_cols))
    gate_wide = jnp.pad(own_weights[0], side_pad)
    up_wide = jnp.pad(own_weights[1], side_pad)
    gate_val = jnp.einsum(
        "desf,hf->desh", column, gate_wide, preferred_element_type=jnp.float32
    )
    up_val = jnp.einsum("desf,hf->desh", column, up_wide, preferred_element_type=jnp.float32)
    hidden = (jax.nn.silu(gate_val) * up_val).astype(jnp.bfloat16)
    hidden_kept = hidden * kept_mask[..., None].astype(jnp.bfloat16)
    unit_count = hidden_kept.shape[-1]
    hidden_block = hidden_kept.reshape(1, groups * experts * slot_cap, unit_count)
    hidden_all = lax.all_to_all(
        jnp.broadcast_to(hidden_block, (groups,) + hidden_block.shape[1:]),
        "dp",
        split_axis=0,
        concat_axis=0,
        tiled=True,
    )
    feature_cols = own_weights[2].shape[1]
    down_split = own_weights[2].reshape(groups, unit_count, feature_cols)
    summed = jnp.einsum(
        "gsn,gnf->sf", hidden_all, down_split, preferred_element_type=jnp.float32
    )
    results = summed.astype(jnp.bfloat16).reshape(groups, experts, slot_cap, feature_cols)
    returned = lax.all_to_all(
        lax.all_to_all(results, "expert", split_axis=1, concat_axis=1, tiled=True),
        "dp",
        split_axis=0,
        concat_axis=3,
        tiled=True,
    )
    returned_flat = returned.reshape(experts * slot_cap, width)
    picked = returned_flat[slot_code]
    expert_mix = jnp.sum(routing_probabilities[:, :, None] * picked.astype(jnp.float32), axis=1)
    layer_out = (stream + expert_mix).astype(jnp.bfloat16)
    gate_held = jnp.where(take_other, partner[0], own_weights[0])
    up_held = jnp.where(take_other, partner[1], own_weights[1])
    down_held = jnp.where(take_other, partner[2], own_weights[2])
    return (layer_out, device_share.reshape(1), gate_held[None], up_held[None], down_held[None])


def solution(mesh):
    in_specs = (
        P(("expert", "dp"), None),
        P(("expert", "dp"), None),
        P(("expert", "dp"), None, None),
        P(("expert", "dp"), None, None),
        P(("expert", "dp"), None),
        P(("expert", "dp"), None),
        P(("expert", "dp")),
        P(),
        P(("expert", "dp"), None),
        P(("expert", "dp"), None),
        P(),
        P(),
        P("expert", "dp", None),
        P("expert", "dp", None),
        P("expert", None, "dp"),
    )
    out_specs = (
        P(("expert", "dp"), None),
        P("expert"),
        P("expert", "dp", None),
        P("expert", "dp", None),
        P("expert", None, "dp"),
    )
    return jax.shard_map(
        per_device, mesh=mesh, in_specs=in_specs, out_specs=out_specs, check_vma=False
    )
```

```python
import jax
import jax.numpy as jnp
from jax import lax
from jax.sharding import PartitionSpec as P

QH = 32
KVH = 4
HEAD = 128


def swapped(value, axis, stride):
    mask = 2**stride
    pairs = [(source, source ^ mask) for source in range(lax.axis_size(axis))]
    return lax.ppermute(value, axis, pairs)


def attention(query_rows, key_rows, value_rows, new_key, new_value, valid_len):
    seq_count = query_rows.shape[0]
    cache_len = key_rows.shape[1]
    group = QH // KVH
    scale = HEAD ** (-0.5)
    query_view = query_rows.reshape(seq_count, KVH, group, HEAD)
    key_view = key_rows.reshape(seq_count, cache_len, KVH, HEAD)
    value_view = value_rows.reshape(seq_count, cache_len, KVH, HEAD)
    scores = (
        jnp.einsum("skgd,slkd->skgl", query_view, key_view, preferred_element_type=jnp.float32)
        * scale
    )
    valid = lax.broadcasted_iota(jnp.int32, (seq_count, cache_len), 1) < valid_len[:, None]
    scores = jnp.where(valid[:, None, None, :], scores, -1e30)
    own_score = (
        jnp.einsum(
            "skgd,skd->skg",
            query_view,
            new_key.reshape(seq_count, KVH, HEAD),
            preferred_element_type=jnp.float32,
        )
        * scale
    )
    highest = jnp.maximum(jnp.max(scores, axis=-1), own_score)
    weights = jnp.exp(scores - highest[..., None])
    own_weight = jnp.exp(own_score - highest)
    denom = jnp.sum(weights, axis=-1) + own_weight
    probs = (weights / denom[..., None]).astype(jnp.bfloat16)
    own_prob = (own_weight / denom).astype(jnp.bfloat16)
    mixed = jnp.einsum("skgl,slkd->skgd", probs, value_view, preferred_element_type=jnp.float32)
    mixed = mixed + own_prob.astype(jnp.float32)[..., None] * new_value.reshape(
        seq_count, KVH, 1, HEAD
    ).astype(jnp.float32)
    return mixed.reshape(seq_count, QH * HEAD).astype(jnp.bfloat16)


def per_device(
    skip_stream,
    attention_probes,
    stored_attention_lookups,
    stored_attention_contents,
    incoming_lookup_entries,
    incoming_content_entries,
    filled_slot_spans,
    layernorm_gain,
    routed_specialist_indices,
    routing_probabilities,
    admission_limits,
    swap_indicator,
    gating_projection_matrix,
    widening_projection_matrix,
    output_projection_matrix,
):
    experts = lax.axis_size("expert")
    groups = lax.axis_size("dp")
    half_axis = experts // 2
    far_bit = experts.bit_length() - 2
    my_index = lax.axis_index("expert")
    my_device = my_index * groups + lax.axis_index("dp")
    own_weights = (
        gating_projection_matrix[0],
        widening_projection_matrix[0],
        output_projection_matrix[0],
    )
    partner = swapped(own_weights, "expert", far_bit)
    take_other = swap_indicator[my_index] == 1
    retained_specialist = jnp.where(take_other, (my_index + half_axis) % experts, my_index)

    seq_rows = skip_stream.shape[0]
    width = skip_stream.shape[1]
    slot_cap = 2
    side_cols = 128
    expert_range = lax.broadcasted_iota(jnp.int32, (experts,), 0)

    attn = attention(
        attention_probes,
        stored_attention_lookups,
        stored_attention_contents,
        incoming_lookup_entries,
        incoming_content_entries,
        filled_slot_spans,
    )
    stream = skip_stream.astype(jnp.float32) + attn.astype(jnp.float32)
    normed = (
        stream
        * lax.rsqrt(jnp.mean(stream * stream, axis=-1, keepdims=True) + 1e-06)
        * layernorm_gain
    ).astype(jnp.bfloat16)

    route_hot = (routed_specialist_indices[:, :, None] == expert_range[None, None, :]).astype(
        jnp.int32
    )
    row_hot = jnp.sum(route_hot, axis=1)
    earlier = jnp.cumsum(row_hot, axis=0) - row_hot
    local_rank = jnp.sum(route_hot * earlier[:, None, :], axis=-1)
    slot_code = routed_specialist_indices * slot_cap + local_rank
    targets = lax.broadcasted_iota(jnp.int32, (experts * slot_cap,), 0)
    slot_hits = jnp.any(slot_code[:, :, None] == targets[None, None, :], axis=1)
    occupied = jnp.any(slot_hits, axis=0)
    row_range = lax.broadcasted_iota(jnp.int32, (seq_rows, 1), 0)
    source_row = jnp.sum(jnp.where(slot_hits, row_range, 0), axis=0) + jnp.where(
        occupied, 0, seq_rows
    )
    padded_rows = jnp.concatenate([normed, jnp.zeros((1, width), jnp.bfloat16)], axis=0)
    outgoing = padded_rows[source_row].reshape(experts, slot_cap, width)
    partner_hist = jnp.roll(jnp.sum(row_hot, axis=0), -half_axis)
    col = lax.broadcasted_iota(jnp.int32, (experts, slot_cap, side_cols), 2)
    slot_of = lax.broadcasted_iota(jnp.int32, (experts, slot_cap, side_cols), 1)
    side = jnp.where(
        col == 0,
        occupied.reshape(experts, slot_cap, 1).astype(jnp.float32),
        jnp.where(
            (col == 1) & (slot_of == 0), partner_hist[:, None, None].astype(jnp.float32), 0.0
        ),
    ).astype(jnp.bfloat16)
    payload = jnp.concatenate([outgoing, side], axis=-1)
    arrived = lax.all_to_all(payload, "expert", split_axis=0, concat_axis=0, tiled=True)
    column = lax.all_to_all(
        jnp.broadcast_to(arrived[None], (groups,) + arrived.shape),
        "dp",
        split_axis=0,
        concat_axis=0,
        tiled=True,
    )
    marks = column[:, :, :, width].astype(jnp.float32)
    partner_total = jnp.sum(column[:, :, :, width + 1].astype(jnp.float32))
    occupied_flat = jnp.transpose(marks, (1, 0, 2)).reshape(-1)
    before_count = jnp.cumsum(occupied_flat) - occupied_flat
    kept_flat = occupied_flat * (
        before_count < admission_limits[my_index].astype(jnp.float32)
    ).astype(jnp.float32)
    kept_mask = jnp.transpose(kept_flat.reshape(experts, groups, slot_cap), (1, 0, 2))
    own_total = jnp.sum(occupied_flat)
    held_tally = jnp.where(take_other, partner_total, own_total)
    device_share = jnp.minimum(
        held_tally, admission_limits[retained_specialist].astype(jnp.float32)
    ) / (seq_rows * routed_specialist_indices.shape[1] * groups)

    side_pad = ((0, 0), (0, side_cols))
    gate_wide = jnp.pad(own_weights[0], side_pad)
    up_wide = jnp.pad(own_weights[1], side_pad)
    gate_val = jnp.einsum(
        "desf,hf->desh", column, gate_wide, preferred_element_type=jnp.float32
    )
    up_val = jnp.einsum("desf,hf->desh", column, up_wide, preferred_element_type=jnp.float32)
    hidden = (jax.nn.silu(gate_val) * up_val).astype(jnp.bfloat16)
    hidden_kept = hidden * kept_mask[..., None].astype(jnp.bfloat16)
    unit_count = hidden_kept.shape[-1]
    hidden_block = hidden_kept.reshape(1, groups * experts * slot_cap, unit_count)
    hidden_all = lax.all_to_all(
        jnp.broadcast_to(hidden_block, (groups,) + hidden_block.shape[1:]),
        "dp",
        split_axis=0,
        concat_axis=0,
        tiled=True,
    )
    feature_cols = own_weights[2].shape[1]
    down_split = own_weights[2].reshape(groups, unit_count, feature_cols)
    summed = jnp.einsum(
        "gsn,gnf->sf", hidden_all, down_split, preferred_element_type=jnp.float32
    )
    results = summed.astype(jnp.bfloat16).reshape(groups, experts, slot_cap, feature_cols)
    joined = lax.all_to_all(results, "dp", split_axis=0, concat_axis=3, tiled=True)[0]
    returned = lax.all_to_all(joined, "expert", split_axis=0, concat_axis=0, tiled=True)
    returned_flat = returned.reshape(experts * slot_cap, width)
    picked = returned_flat[slot_code]
    expert_mix = jnp.sum(routing_probabilities[:, :, None] * picked.astype(jnp.float32), axis=1)
    layer_out = (stream + expert_mix).astype(jnp.bfloat16)
    gate_held = jnp.where(take_other, partner[0], own_weights[0])
    up_held = jnp.where(take_other, partner[1], own_weights[1])
    down_held = jnp.where(take_other, partner[2], own_weights[2])
    return (layer_out, device_share.reshape(1), gate_held[None], up_held[None], down_held[None])


def solution(mesh):
    in_specs = (
        P(("expert", "dp"), None),
        P(("expert", "dp"), None),
        P(("expert", "dp"), None, None),
        P(("expert", "dp"), None, None),
        P(("expert", "dp"), None),
        P(("expert", "dp"), None),
        P(("expert", "dp")),
        P(),
        P(("expert", "dp"), None),
        P(("expert", "dp"), None),
        P(),
        P(),
        P("expert", "dp", None),
        P("expert", "dp", None),
        P("expert", None, "dp"),
    )
    out_specs = (
        P(("expert", "dp"), None),
        P("expert"),
        P("expert", "dp", None),
        P("expert", "dp", None),
        P("expert", None, "dp"),
    )
    return jax.shard_map(
        per_device, mesh=mesh, in_specs=in_specs, out_specs=out_specs, check_vma=False
    )
```
